256 devices in a mesh: dp: 16 (over y, x), expert: 16 (over z, core).
Axes of the slice: x: 4, y: 4, z: 8, core: 2. Of those that a mesh axis runs over, the one named last changes fastest.
Arguments:
- tokens: bfloat16 [32768, 768], P(('dp', 'expert')), may hold values from -6 to 6
- cotangent: bfloat16 [32768, 768], P(('dp', 'expert')), may hold values from -6 to 6
- routes: int32 [32768, 2], P(('dp', 'expert')), may hold values from 0 to 15, all different within a row; in each aligned block of 128 rows (0 to 127, 128 to 255, ...) at most 48 rows name the same one
- gates: float32 [32768, 2], P(('dp', 'expert')), may hold values from 0.1 to 1
- w_in: bfloat16 [16, 2304, 768], P('expert', 'dp'), may hold values from -0.21875 to 0.21875
- w_out: bfloat16 [16, 2304, 768], P('expert', 'dp'), may hold values from -0.125 to 0.125
Outputs:
- d_tokens: bfloat16 [32768, 768], P(('dp', 'expert'))
- grad_in: float32 [16, 2304, 768], P('expert', 'dp')
- grad_out: float32 [16, 2304, 768], P('expert', 'dp')
The draws below stay inside these ranges and needn't reach their ends.
Inputs may be any that keep to these rules, and one draw needn't show every extreme that they name: `routes`: within the rows of one device (128 rows) no expert is named more than 48 times, and in every draw some expert is named exactly 48 times by the rows of some device; the 2 entries of a row differ.
All inputs are finite; a program needn't handle non-finite values.
Results may differ from the reference program's by a relative error of at most 0.015.
Values may be sent and summed in bfloat16 or wider, within the bound.
No kernel may reach another device: no remote copies, remote signals or barrier semaphores. Data moves between devices by JAX's collectives and lax.ppermute only.
A program may use at most 64 MiB of HBM per device.

```python
import math
import jax
import jax.numpy as jnp
import numpy as np
from jax import lax

D = 768
HID = 2304
TOPK = 2
TOK_DEV = 128
EXPERTS = 16
CAP = 48
TOKENS = 32768
N_DP = 16


def block_levels(stream_key, dims, split, least, high):
    def one(axis_at, shards_of):
        heights = jax.random.uniform(jax.random.fold_in(jax.random.fold_in(stream_key, 6), axis_at), (shards_of,), jnp.float32, least / len(split), high / len(split))
        return jnp.repeat(jnp.exp(heights), dims[axis_at] // shards_of).reshape((-1,) + (1,) * (len(dims) - axis_at - 1))

    factor_of = one(*split[0])
    for cut in split[1:]:
        factor_of = factor_of * one(*cut)
    return factor_of


def assign_block(rng, own, number, rows, amount, top, most, skew):
    sequence = jax.random.permutation(rng, amount)
    crowded, common = shares(amount, rows * top, most, skew, True), shares(amount, rows * top, most, skew, False)
    places = jnp.arange(amount)

    def named(tallies, rotation):
        used = int((tallies > 0).sum())
        fixed = max(1, used // 4)
        shifted = fixed + (places - fixed + rotation * (used - fixed)) % max(1, amount - fixed)
        return jnp.zeros((amount,), jnp.int32).at[sequence[jnp.where(places < fixed, places, shifted)]].set(jnp.asarray(tallies, jnp.int32))

    tallies = jnp.where(number % 4 == 0, named(crowded, number // 4), named(common, number - number // 4 - 1))
    mixed = jax.random.permutation(jax.random.fold_in(own, 3), amount)
    giver, taker = mixed[0:amount // 2 * 2:2], mixed[1:amount // 2 * 2:2]
    slack = jnp.minimum(tallies[giver] - 1, most - tallies[taker]) // 2
    slack = jnp.where((giver == sequence[0]) | (taker == sequence[0]) | (tallies[taker] == 0), 0, jnp.maximum(slack, 0))
    shifted = jax.random.randint(jax.random.fold_in(own, 4), (amount // 2,), 0, 1 << 20) % (slack + 1)
    tallies = tallies.at[giver].add(-shifted).at[taker].add(shifted)
    labels = jnp.searchsorted(jnp.cumsum(tallies), jnp.arange(rows * top), side="right").astype(jnp.int32)
    table = labels.reshape(top, rows).T
    table = table[jax.random.permutation(jax.random.fold_in(own, 1), rows)]
    rotation = jax.random.randint(jax.random.fold_in(own, 2), (rows, 1), 0, top)
    return jnp.take_along_axis(table, (jnp.arange(top)[None, :] + rotation) % top, axis=1)


def shares(count, total, bound, slope, full):
    weights = [(1 << 20) // math.isqrt(standing ** slope) + 1 for standing in range(1, count + 1)]
    largest = bound if full else min(bound, max(-(-total // count), total * weights[0] // sum(weights)))
    least = 1 if total - largest >= count - 1 else 0
    counts, rest = [largest] + [least] * (count - 1), total - largest - least * (count - 1)
    while rest > 0:
        free = [i for i in range(1, count) if counts[i] < largest] or [i for i in range(1, count) if counts[i] < bound]
        mass, budget = sum([weights[i] for i in free]), rest
        for i in free:
            extra = min(bound - counts[i], max(1, budget * weights[i] // mass), rest)
            counts[i] = counts[i] + extra
            rest = rest - extra
    return np.array(counts)


def gaussian(rng, extent, scale, limit, pieces=(), kind=jnp.bfloat16):
    array = jax.random.normal(rng, extent, jnp.float32) * scale
    if len(pieces) > 0:
        array = block_levels(rng, extent, pieces, -0.22, 0.18) * array
    return jnp.clip(array, min=-limit, max=limit).astype(kind)


def setup_inputs(seed: int = 0) -> dict:
    arg_keys = jax.random.split(jax.random.key(seed), 7)
    tokens = gaussian(arg_keys[0], (TOKENS, D), 1.0, 6.0, ((0, 256),))
    cotangent = gaussian(arg_keys[1], (TOKENS, D), 1.0, 6.0, ((0, 256),))
    routes_keys = jax.random.split(jax.random.fold_in(arg_keys[2], 1), TOKENS // TOK_DEV)
    routes_turns = jax.random.permutation(jax.random.fold_in(arg_keys[2], 3), TOKENS // TOK_DEV)
    routes = jax.vmap(lambda own, number: assign_block(jax.random.fold_in(arg_keys[2], 2), own, number, TOK_DEV, EXPERTS, TOPK, CAP, 2))(routes_keys, routes_turns).reshape((TOKENS, TOPK))
    gates = jnp.clip(jnp.exp(math.log(1.0) - 2.3025851 * jax.random.uniform(arg_keys[3], (TOKENS, TOPK), jnp.float32) ** block_levels(arg_keys[3], (TOKENS, TOPK), ((0, 256),), -0.2, 0.2)), 0.1, 1.0)
    w_in = gaussian(arg_keys[4], (EXPERTS, HID, D), D ** -0.5, 0.21875, ((0, 16), (1, 16)))
    w_out = gaussian(arg_keys[5], (EXPERTS, HID, D), HID ** -0.5, 0.125, ((0, 16), (1, 16)))
    return {"tokens": tokens, "cotangent": cotangent, "routes": routes, "gates": gates, "w_in": w_in, "w_out": w_out}


tanh_coef = 0.7978845608028654
cubic_coef = 0.044715


def gelu_tanh(value):
    inner = tanh_coef * (value + cubic_coef * value * value * value)
    return 0.5 * value * (1.0 + jnp.tanh(inner))


def gelu_slope(value):
    inner = tanh_coef * (value + cubic_coef * value * value * value)
    slope_t = jnp.tanh(inner)
    return 0.5 * (1.0 + slope_t) + 0.5 * value * (1.0 - slope_t * slope_t) * tanh_coef * (1.0 + 3.0 * cubic_coef * value * value)


def dispatch_tables(route_blk, gate_blk, experts, capacity):
    tok_rows = route_blk.shape[0]
    flat = route_blk.reshape(-1)
    onehot = (flat[:, None] == jnp.arange(experts, dtype=jnp.int32)[None, :]).astype(jnp.int32)
    before = jnp.cumsum(onehot, axis=0) - onehot
    position = jnp.sum(before * onehot, axis=1).astype(jnp.int32)
    slots = (flat * capacity + position).reshape(tok_rows, -1)
    slot_ids = jnp.arange(experts * capacity, dtype=jnp.int32)
    placed = slot_ids[:, None, None] == slots[None, :, :]
    route_mat = jnp.sum(placed.astype(jnp.float32), axis=2)
    gate_slot = jnp.sum(jnp.where(placed, gate_blk[None, :, :], jnp.float32(0.0)), axis=(1, 2))
    return route_mat, gate_slot


def expert_backward(operands):
    rows_in, grads_in, weight_in, weight_out = operands
    weight_in32 = weight_in.astype(jnp.float32)
    weight_out32 = weight_out.astype(jnp.float32)
    rows32 = rows_in.astype(jnp.float32)
    grads32 = grads_in.astype(jnp.float32)
    pre = jnp.dot(rows32, weight_in32.T)
    acts = gelu_tanh(pre).astype(jnp.bfloat16)
    grad_act = jnp.dot(grads32, weight_out32.T)
    dpre = (grad_act * gelu_slope(pre)).astype(jnp.bfloat16)
    dpre32 = dpre.astype(jnp.float32)
    slot_grads = jnp.dot(dpre32, weight_in32).astype(jnp.bfloat16)
    part_in = jnp.dot(dpre32.T, rows32).astype(jnp.bfloat16)
    part_out = jnp.dot(acts.astype(jnp.float32).T, grads32).astype(jnp.bfloat16)
    return slot_grads, part_in, part_out


def reference(tokens, cotangent, routes, gates, w_in, w_out):
    sources = EXPERTS
    tok_all = tokens.reshape(N_DP, sources, TOK_DEV, D)
    cot_all = cotangent.reshape(N_DP, sources, TOK_DEV, D)
    route_all = routes.reshape(N_DP, sources, TOK_DEV, TOPK)
    gate_all = gates.reshape(N_DP, sources, TOK_DEV, TOPK)

    def row_group(state_now, inputs):
        tok_blk, cot_blk, route_blk, gate_blk = inputs
        route_mat, gate_slot = jax.vmap(lambda rr, gg: dispatch_tables(rr, gg, EXPERTS, CAP))(route_blk, gate_blk)
        rows_sent = jnp.einsum("sct,std->scd", route_mat, tok_blk.astype(jnp.float32)).astype(jnp.bfloat16)
        grad_rows = jnp.einsum("sct,std->scd", route_mat, cot_blk.astype(jnp.float32))
        grads_sent = (gate_slot[:, :, None] * grad_rows).astype(jnp.bfloat16)
        rows_expert = rows_sent.reshape(sources, EXPERTS, CAP, D).transpose(1, 0, 2, 3).reshape(EXPERTS, sources * CAP, D)
        grads_expert = grads_sent.reshape(sources, EXPERTS, CAP, D).transpose(1, 0, 2, 3).reshape(EXPERTS, sources * CAP, D)
        slot_grads, part_in, part_out = lax.map(expert_backward, (rows_expert, grads_expert, w_in, w_out))
        returned = slot_grads.reshape(EXPERTS, sources, CAP, D).transpose(1, 0, 2, 3).reshape(sources, EXPERTS * CAP, D)
        token_grads = jnp.einsum("sct,scd->std", route_mat, returned.astype(jnp.float32)).astype(jnp.bfloat16)
        new_state = (state_now[0] + part_in.astype(jnp.float32), state_now[1] + part_out.astype(jnp.float32))
        return new_state, token_grads

    zero_grads = jnp.zeros((EXPERTS, HID, D), jnp.float32)
    (grad_in, grad_out), token_grads = lax.scan(row_group, (zero_grads, zero_grads), (tok_all, cot_all, route_all, gate_all))
    d_tokens = token_grads.reshape(TOKENS, D)
    return d_tokens, grad_in, grad_out
```

```python
import jax
import jax.numpy as jnp
from jax import lax
from jax.sharding import PartitionSpec as P

tanh_coef = 0.7978845608028654
cubic_coef = 0.044715


def gelu_tanh(value):
    inner = tanh_coef * (value + cubic_coef * value * value * value)
    return 0.5 * value * (1.0 + jnp.tanh(inner))


def gelu_slope(value):
    inner = tanh_coef * (value + cubic_coef * value * value * value)
    slope_t = jnp.tanh(inner)
    return 0.5 * (1.0 + slope_t) + 0.5 * value * (1.0 - slope_t * slope_t) * tanh_coef * (
        1.0 + 3.0 * cubic_coef * value * value
    )


def dispatch_tables(route_blk, gate_blk, experts, capacity):
    tok_rows = route_blk.shape[0]
    flat = route_blk.reshape(-1)
    onehot = (flat[:, None] == jnp.arange(experts, dtype=jnp.int32)[None, :]).astype(jnp.int32)
    before = jnp.cumsum(onehot, axis=0) - onehot
    position = jnp.sum(before * onehot, axis=1)
    slots = (flat * capacity + position).reshape(tok_rows, -1)
    slot_ids = jnp.arange(experts * capacity, dtype=jnp.int32)
    placed = slot_ids[:, None, None] == slots[None, :, :]
    route_mat = jnp.sum(placed.astype(jnp.int32), axis=2).astype(jnp.bfloat16)
    gate_slot = jnp.sum(jnp.where(placed, gate_blk[None, :, :], jnp.float32(0.0)), axis=(1, 2))
    return (route_mat, gate_slot)


def shards(tokens, cotangent, routes, gates, w_in, w_out):
    experts = lax.axis_size("expert")
    tok_rows, model_width = tokens.shape
    top_count = routes.shape[1]
    capacity = 3 * tok_rows * top_count // experts
    shard_rows = w_in.shape[1]
    slot_rows = experts * capacity
    route_mat, gate_slot = dispatch_tables(routes, gates, experts, capacity)
    rows_sent = jnp.dot(route_mat, tokens, preferred_element_type=jnp.float32).astype(jnp.bfloat16)
    grad_rows = jnp.dot(route_mat, cotangent, preferred_element_type=jnp.float32)
    grads_sent = (gate_slot[:, None] * grad_rows).astype(jnp.bfloat16)
    both_sent = jnp.stack(
        [rows_sent.reshape(experts, capacity, model_width), grads_sent.reshape(experts, capacity, model_width)],
        axis=1,
    )
    both_recv = lax.all_to_all(both_sent, "expert", split_axis=0, concat_axis=0, tiled=True)
    rows_in = both_recv[:, 0].reshape(slot_rows, model_width)
    grads_in = both_recv[:, 1].reshape(slot_rows, model_width)
    piece_in = lax.all_gather(w_in[0], "dp", axis=0, tiled=True)
    piece_out = lax.all_gather(w_out[0], "dp", axis=0, tiled=True)
    pre = lax.dot_general(
        rows_in, piece_in, (((1,), (1,)), ((), ())), preferred_element_type=jnp.float32
    )
    acts = gelu_tanh(pre).astype(jnp.bfloat16)
    grad_act = lax.dot_general(
        grads_in, piece_out, (((1,), (1,)), ((), ())), preferred_element_type=jnp.float32
    )
    dpre = (grad_act * gelu_slope(pre)).astype(jnp.bfloat16)
    slot_sum = jnp.dot(dpre, piece_in, preferred_element_type=jnp.float32)
    slot_sum, acts_all, dpre_all = (slot_sum, acts, dpre)
    returned = lax.all_to_all(
        slot_sum.astype(jnp.bfloat16).reshape(experts, capacity, model_width),
        "expert",
        split_axis=0,
        concat_axis=0,
        tiled=True,
    )
    token_grads = lax.dot_general(
        route_mat,
        returned.reshape(slot_rows, model_width),
        (((0,), (0,)), ((), ())),
        preferred_element_type=jnp.float32,
    )
    d_tokens = token_grads.astype(jnp.bfloat16)
    term_in = lax.dot_general(
        dpre_all, rows_in, (((0,), (0,)), ((), ())), preferred_element_type=jnp.float32
    )
    term_out = lax.dot_general(
        acts_all, grads_in, (((0,), (0,)), ((), ())), preferred_element_type=jnp.float32
    )
    grad_in = lax.psum_scatter(term_in.astype(jnp.bfloat16), "dp", scatter_dimension=0, tiled=True)
    grad_out = lax.psum_scatter(term_out.astype(jnp.bfloat16), "dp", scatter_dimension=0, tiled=True)
    grad_in = grad_in.astype(jnp.float32)[None]
    grad_out = grad_out.astype(jnp.float32)[None]
    return (d_tokens, grad_in, grad_out)


def solution(mesh):
    in_specs = (
        P(("dp", "expert"), None),
        P(("dp", "expert"), None),
        P(("dp", "expert"), None),
        P(("dp", "expert"), None),
        P("expert", "dp", None),
        P("expert", "dp", None),
    )
    out_specs = (P(("dp", "expert"), None), P("expert", "dp", None), P("expert", "dp", None))
    return jax.shard_map(shards, mesh=mesh, in_specs=in_specs, out_specs=out_specs, check_vma=False)
```

```python
import jax
import jax.numpy as jnp
from jax import lax
from jax.sharding import PartitionSpec as P

tanh_coef = 0.7978845608028654
cubic_coef = 0.044715


def gelu_tanh(value):
    inner = tanh_coef * (value + cubic_coef * value * value * value)
    return 0.5 * value * (1.0 + jnp.tanh(inner))


def gelu_slope(value):
    inner = tanh_coef * (value + cubic_coef * value * value * value)
    slope_t = jnp.tanh(inner)
    return 0.5 * (1.0 + slope_t) + 0.5 * value * (1.0 - slope_t * slope_t) * tanh_coef * (
        1.0 + 3.0 * cubic_coef * value * value
    )


def dispatch_tables(route_blk, gate_blk, experts, capacity):
    tok_rows = route_blk.shape[0]
    flat = route_blk.reshape(-1)
    onehot = (flat[:, None] == jnp.arange(experts, dtype=jnp.int32)[None, :]).astype(jnp.int32)
    before = jnp.cumsum(onehot, axis=0) - onehot
    position = jnp.sum(before * onehot, axis=1)
    slots = (flat * capacity + position).reshape(tok_rows, -1)
    slot_ids = jnp.arange(experts * capacity, dtype=jnp.int32)
    placed = slot_ids[:, None, None] == slots[None, :, :]
    route_mat = jnp.sum(placed.astype(jnp.int32), axis=2).astype(jnp.bfloat16)
    gate_slot = jnp.sum(jnp.where(placed, gate_blk[None, :, :], jnp.float32(0.0)), axis=(1, 2))
    return (route_mat, gate_slot)


def grid_perm(ny, nx, dim, sign):
    pairs = []
    for d in range(ny * nx):
        cy, cx = divmod(d, nx)
        if dim == "x":
            pairs.append((d, cy * nx + (cx + sign) % nx))
        else:
            pairs.append((d, ((cy + sign) % ny) * nx + cx))
    return pairs


def ring_gather(piece, n, perm, sign):
    got = [None] * n
    got[0] = piece
    cur = piece
    for s in range(n - 1):
        cur = lax.ppermute(cur, "dp", perm)
        got[(sign * (s + 1)) % n] = cur
    return got


def ring_reduce(blocks, n, perm, sign):
    acc = blocks[sign % n]
    for s in range(n - 1):
        sent = jax.tree.map(lambda a: a.astype(jnp.bfloat16), acc)
        recv = lax.ppermute(sent, "dp", perm)
        add = blocks[(sign * (s + 2)) % n]
        acc = jax.tree.map(lambda r, b: r.astype(jnp.float32) + b, recv, add)
    return acc


def stream_specs(ny, nx, rows, cols):
    half_r, half_c = rows // 2, cols // 2
    return [
        (slice(0, half_r), slice(0, half_c), ("x", 1), ("y", 1)),
        (slice(half_r, rows), slice(0, half_c), ("x", -1), ("y", -1)),
        (slice(0, half_r), slice(half_c, cols), ("y", 1), ("x", 1)),
        (slice(half_r, rows), slice(half_c, cols), ("y", -1), ("x", -1)),
    ]


def grid_all_gather(shards, ny, nx):
    rows, cols = shards[0].shape
    sizes = {"x": nx, "y": ny}
    quads = {}
    for rs, cs, first, second in stream_specs(ny, nx, rows, cols):
        piece = tuple(w[rs, cs] for w in shards)
        g1 = ring_gather(piece, sizes[first[0]], grid_perm(ny, nx, *first), first[1])
        stack1 = tuple(jnp.stack([g[i] for g in g1]) for i in range(len(shards)))
        g2 = ring_gather(stack1, sizes[second[0]], grid_perm(ny, nx, *second), second[1])
        full = tuple(jnp.stack([g[i] for g in g2]) for i in range(len(shards)))
        if first[0] == "x":
            full = tuple(jnp.swapaxes(f, 0, 1) for f in full)
        quads[(rs.start, cs.start)] = full
    half_r, half_c = rows // 2, cols // 2
    out = []
    for i in range(len(shards)):
        top = jnp.concatenate([quads[(0, 0)][i], quads[(0, half_c)][i]], axis=3)
        bottom = jnp.concatenate([quads[(half_r, 0)][i], quads[(half_r, half_c)][i]], axis=3)
        out.append(jnp.concatenate([top, bottom], axis=2))
    return tuple(out)


def grid_reduce_scatter(terms, ny, nx):
    _, _, rows, cols = terms[0].shape
    sizes = {"x": nx, "y": ny}
    quads = {}
    for rs, cs, first, second in stream_specs(ny, nx, rows, cols):
        n1, n2 = sizes[first[0]], sizes[second[0]]
        if first[0] == "x":
            blocks = [tuple(t[k, :, rs, cs] for t in terms) for k in range(n1)]
        else:
            blocks = [tuple(t[:, k, rs, cs] for t in terms) for k in range(n1)]
        part = ring_reduce(blocks, n1, grid_perm(ny, nx, *first), first[1])
        blocks2 = [tuple(p[k] for p in part) for k in range(n2)]
        quads[(rs.start, cs.start)] = ring_reduce(blocks2, n2, grid_perm(ny, nx, *second), second[1])
    half_r, half_c = rows // 2, cols // 2
    out = []
    for i in range(len(terms)):
        top = jnp.concatenate([quads[(0, 0)][i], quads[(0, half_c)][i]], axis=1)
        bottom = jnp.concatenate([quads[(half_r, 0)][i], quads[(half_r, half_c)][i]], axis=1)
        out.append(jnp.concatenate([top, bottom], axis=0))
    return tuple(out)


def make_shards(ny, nx):
    def shards(tokens, cotangent, routes, gates, w_in, w_out):
        experts = lax.axis_size("expert")
        tok_rows, model_width = tokens.shape
        top_count = routes.shape[1]
        capacity = 3 * tok_rows * top_count // experts
        shard_rows = w_in.shape[1]
        slot_rows = experts * capacity
        route_mat, gate_slot = dispatch_tables(routes, gates, experts, capacity)
        rows_sent = jnp.dot(route_mat, tokens, preferred_element_type=jnp.float32).astype(jnp.bfloat16)
        grad_rows = jnp.dot(route_mat, cotangent, preferred_element_type=jnp.float32)
        grads_sent = (gate_slot[:, None] * grad_rows).astype(jnp.bfloat16)
        rows_recv, grads_recv = (
            lax.all_to_all(
                rows_sent.reshape(experts, capacity, model_width), "expert", split_axis=0, concat_axis=0, tiled=True
            ),
            lax.all_to_all(
                grads_sent.reshape(experts, capacity, model_width), "expert", split_axis=0, concat_axis=0, tiled=True
            ),
        )
        rows_in = rows_recv.reshape(slot_rows, model_width)
        grads_in = grads_recv.reshape(slot_rows, model_width)
        full_in, full_out = grid_all_gather((w_in[0], w_out[0]), ny, nx)
        hidden = nx * ny * shard_rows
        piece_in = full_in.reshape(hidden, model_width)
        piece_out = full_out.reshape(hidden, model_width)
        pre = lax.dot_general(
            rows_in, piece_in, (((1,), (1,)), ((), ())), preferred_element_type=jnp.float32
        )
        acts = gelu_tanh(pre).astype(jnp.bfloat16)
        grad_act = lax.dot_general(
            grads_in, piece_out, (((1,), (1,)), ((), ())), preferred_element_type=jnp.float32
        )
        dpre = (grad_act * gelu_slope(pre)).astype(jnp.bfloat16)
        slot_sum = jnp.dot(dpre, piece_in, preferred_element_type=jnp.float32)
        returned = lax.all_to_all(
            slot_sum.astype(jnp.bfloat16).reshape(experts, capacity, model_width),
            "expert",
            split_axis=0,
            concat_axis=0,
            tiled=True,
        )
        token_grads = lax.dot_general(
            route_mat,
            returned.reshape(slot_rows, model_width),
            (((0,), (0,)), ((), ())),
            preferred_element_type=jnp.float32,
        )
        d_tokens = token_grads.astype(jnp.bfloat16)
        term_in = lax.dot_general(
            dpre, rows_in, (((0,), (0,)), ((), ())), preferred_element_type=jnp.float32
        )
        term_out = lax.dot_general(
            acts, grads_in, (((0,), (0,)), ((), ())), preferred_element_type=jnp.float32
        )
        term_in = term_in.astype(jnp.bfloat16).astype(jnp.float32)
        term_out = term_out.astype(jnp.bfloat16).astype(jnp.float32)
        grid_shape = (nx, ny, shard_rows, model_width)
        grad_in, grad_out = grid_reduce_scatter(
            (term_in.reshape(grid_shape), term_out.reshape(grid_shape)), ny, nx
        )
        return (d_tokens, grad_in[None], grad_out[None])

    return shards


def solution(mesh):
    axis_sizes = {}
    for name, size in zip(mesh.axis_names, mesh.devices.shape):
        axis_sizes[name] = size
    n_dp = axis_sizes["dp"]
    nx = 4 if n_dp % 4 == 0 else 1
    ny = n_dp // nx
    in_specs = (
        P(("dp", "expert"), None),
        P(("dp", "expert"), None),
        P(("dp", "expert"), None),
        P(("dp", "expert"), None),
        P("expert", "dp", None),
        P("expert", "dp", None),
    )
    out_specs = (P(("dp", "expert"), None), P("expert", "dp", None), P("expert", "dp", None))
    return jax.shard_map(
        make_shards(ny, nx), mesh=mesh, in_specs=in_specs, out_specs=out_specs, check_vma=False
    )
```

```python
import jax
import jax.numpy as jnp
from jax import lax
from jax.sharding import PartitionSpec as P

tanh_coef = 0.7978845608028654
cubic_coef = 0.044715


def gelu_tanh(value):
    inner = tanh_coef * (value + cubic_coef * value * value * value)
    return 0.5 * value * (1.0 + jnp.tanh(inner))


def gelu_slope(value):
    inner = tanh_coef * (value + cubic_coef * value * value * value)
    slope_t = jnp.tanh(inner)
    return 0.5 * (1.0 + slope_t) + 0.5 * value * (1.0 - slope_t * slope_t) * tanh_coef * (
        1.0 + 3.0 * cubic_coef * value * value
    )


def dispatch_tables(route_blk, gate_blk, experts, capacity):
    tok_rows = route_blk.shape[0]
    flat = route_blk.reshape(-1)
    onehot = (flat[:, None] == jnp.arange(experts, dtype=jnp.int32)[None, :]).astype(jnp.int32)
    before = jnp.cumsum(onehot, axis=0) - onehot
    position = jnp.sum(before * onehot, axis=1)
    slots = (flat * capacity + position).reshape(tok_rows, -1)
    slot_ids = jnp.arange(experts * capacity, dtype=jnp.int32)
    placed = slot_ids[:, None, None] == slots[None, :, :]
    route_mat = jnp.sum(placed.astype(jnp.int32), axis=2).astype(jnp.bfloat16)
    gate_slot = jnp.sum(jnp.where(placed, gate_blk[None, :, :], jnp.float32(0.0)), axis=(1, 2))
    return (route_mat, gate_slot)


def shards(tokens, cotangent, routes, gates, w_in, w_out):
    experts = lax.axis_size("expert")
    tok_rows, model_width = tokens.shape
    top_count = routes.shape[1]
    capacity = 3 * tok_rows * top_count // experts
    shard_rows = w_in.shape[1]
    slot_rows = experts * capacity
    route_mat, gate_slot = dispatch_tables(routes, gates, experts, capacity)
    rows_sent = jnp.dot(route_mat, tokens, preferred_element_type=jnp.float32).astype(jnp.bfloat16)
    grad_rows = jnp.dot(route_mat, cotangent, preferred_element_type=jnp.float32)
    grads_sent = (gate_slot[:, None] * grad_rows).astype(jnp.bfloat16)
    both_sent = jnp.stack(
        [rows_sent.reshape(experts, capacity, model_width), grads_sent.reshape(experts, capacity, model_width)],
        axis=1,
    )
    both_recv = lax.all_to_all(both_sent, "expert", split_axis=0, concat_axis=0, tiled=True)
    rows_in = both_recv[:, 0].reshape(slot_rows, model_width)
    grads_in = both_recv[:, 1].reshape(slot_rows, model_width)
    piece_in = lax.all_gather(w_in[0], "dp", axis=0, tiled=True)
    piece_out = lax.all_gather(w_out[0], "dp", axis=0, tiled=True)
    pre = lax.dot_general(
        rows_in, piece_in, (((1,), (1,)), ((), ())), preferred_element_type=jnp.float32
    )
    acts = gelu_tanh(pre).astype(jnp.bfloat16)
    grad_act = lax.dot_general(
        grads_in, piece_out, (((1,), (1,)), ((), ())), preferred_element_type=jnp.float32
    )
    dpre = (grad_act * gelu_slope(pre)).astype(jnp.bfloat16)
    slot_sum = jnp.dot(dpre, piece_in, preferred_element_type=jnp.float32)
    slot_sum, acts_all, dpre_all = (slot_sum, acts, dpre)
    returned = lax.all_to_all(
        slot_sum.astype(jnp.bfloat16).reshape(experts, capacity, model_width),
        "expert",
        split_axis=0,
        concat_axis=0,
        tiled=True,
    )
    token_grads = lax.dot_general(
        route_mat,
        returned.reshape(slot_rows, model_width),
        (((0,), (0,)), ((), ())),
        preferred_element_type=jnp.float32,
    )
    d_tokens = token_grads.astype(jnp.bfloat16)
    term_in = lax.dot_general(
        dpre_all, rows_in, (((0,), (0,)), ((), ())), preferred_element_type=jnp.float32
    )
    term_out = lax.dot_general(
        acts_all, grads_in, (((0,), (0,)), ((), ())), preferred_element_type=jnp.float32
    )
    n_dp = lax.axis_size("dp")
    grad_in = lax.psum_scatter(term_in.astype(jnp.bfloat16), "dp", scatter_dimension=0, tiled=True)
    grad_in = grad_in.astype(jnp.float32)[None]
    parts_out = lax.all_to_all(
        term_out.astype(jnp.bfloat16).reshape(n_dp, shard_rows, model_width),
        "dp",
        split_axis=0,
        concat_axis=0,
        tiled=True,
    )
    grad_out = jnp.sum(parts_out.astype(jnp.float32), axis=0)[None]
    return (d_tokens, grad_in, grad_out)


def solution(mesh):
    in_specs = (
        P(("dp", "expert"), None),
        P(("dp", "expert"), None),
        P(("dp", "expert"), None),
        P(("dp", "expert"), None),
        P("expert", "dp", None),
        P("expert", "dp", None),
    )
    out_specs = (P(("dp", "expert"), None), P("expert", "dp", None), P("expert", "dp", None))
    return jax.shard_map(shards, mesh=mesh, in_specs=in_specs, out_specs=out_specs, check_vma=False)
```

```python
import jax
import jax.numpy as jnp
from jax import lax
from jax.sharding import PartitionSpec as P

tanh_coef = 0.7978845608028654
cubic_coef = 0.044715


def gelu_tanh(value):
    inner = tanh_coef * (value + cubic_coef * value * value * value)
    return 0.5 * value * (1.0 + jnp.tanh(inner))


def gelu_slope(value):
    inner = tanh_coef * (value + cubic_coef * value * value * value)
    slope_t = jnp.tanh(inner)
    return 0.5 * (1.0 + slope_t) + 0.5 * value * (1.0 - slope_t * slope_t) * tanh_coef * (
        1.0 + 3.0 * cubic_coef * value * value
    )


def dispatch_tables(route_blk, gate_blk, experts, capacity):
    tok_rows = route_blk.shape[0]
    flat = route_blk.reshape(-1)
    onehot = (flat[:, None] == jnp.arange(experts, dtype=jnp.int32)[None, :]).astype(jnp.int32)
    before = jnp.cumsum(onehot, axis=0) - onehot
    position = jnp.sum(before * onehot, axis=1)
    slots = (flat * capacity + position).reshape(tok_rows, -1)
    slot_ids = jnp.arange(experts * capacity, dtype=jnp.int32)
    placed = slot_ids[:, None, None] == slots[None, :, :]
    route_mat = jnp.sum(placed.astype(jnp.int32), axis=2).astype(jnp.bfloat16)
    gate_slot = jnp.sum(jnp.where(placed, gate_blk[None, :, :], jnp.float32(0.0)), axis=(1, 2))
    return (route_mat, gate_slot)


def grid_perm(ny, nx, dim, sign):
    pairs = []
    for d in range(ny * nx):
        cy, cx = divmod(d, nx)
        if dim == "x":
            pairs.append((d, cy * nx + (cx + sign) % nx))
        else:
            pairs.append((d, ((cy + sign) % ny) * nx + cx))
    return pairs


def ring_gather(piece, n, perm, sign):
    got = [None] * n
    got[0] = piece
    cur = piece
    for s in range(n - 1):
        cur = lax.ppermute(cur, "dp", perm)
        got[(sign * (s + 1)) % n] = cur
    return jnp.stack(got)


def grid_gather(piece, ny, nx, first, second):
    sizes = {"x": nx, "y": ny}
    g1 = ring_gather(piece, sizes[first[0]], grid_perm(ny, nx, *first), first[1])
    g2 = ring_gather(g1, sizes[second[0]], grid_perm(ny, nx, *second), second[1])
    if first[0] == "x":
        g2 = jnp.swapaxes(g2, 0, 1)
    return g2


def natural_order(rel, ny, nx):
    me = lax.axis_index("dp")
    cy, cx = me // nx, me % nx
    dy, dx = jnp.divmod(jnp.arange(ny * nx, dtype=jnp.int32), nx)
    index = ((cx - dx) % nx) * ny + (cy - dy) % ny
    flat = rel.reshape(nx * ny, rel.shape[2], rel.shape[3])
    return jnp.take(flat, index, axis=0).reshape(-1, rel.shape[3])


def gather_weights(w_in, w_out, ny, nx):
    half = w_in.shape[0] // 2
    in_a = grid_gather(w_in[:half], ny, nx, ("x", 1), ("y", 1))
    in_b = grid_gather(w_in[half:], ny, nx, ("x", -1), ("y", -1))
    out_a = grid_gather(w_out[:half], ny, nx, ("y", 1), ("x", 1))
    out_b = grid_gather(w_out[half:], ny, nx, ("y", -1), ("x", -1))
    full_in = natural_order(jnp.concatenate([in_a, in_b], axis=2), ny, nx)
    full_out = natural_order(jnp.concatenate([out_a, out_b], axis=2), ny, nx)
    return full_in, full_out


def shards(tokens, cotangent, routes, gates, w_in, w_out):
    experts = lax.axis_size("expert")
    tok_rows, model_width = tokens.shape
    top_count = routes.shape[1]
    capacity = 3 * tok_rows * top_count // experts
    shard_rows = w_in.shape[1]
    slot_rows = experts * capacity
    route_mat, gate_slot = dispatch_tables(routes, gates, experts, capacity)
    rows_sent = jnp.dot(route_mat, tokens, preferred_element_type=jnp.float32).astype(jnp.bfloat16)
    grad_rows = jnp.dot(route_mat, cotangent, preferred_element_type=jnp.float32)
    grads_sent = (gate_slot[:, None] * grad_rows).astype(jnp.bfloat16)
    both_sent = jnp.stack(
        [rows_sent.reshape(experts, capacity, model_width), grads_sent.reshape(experts, capacity, model_width)],
        axis=1,
    )
    both_recv = lax.all_to_all(both_sent, "expert", split_axis=0, concat_axis=0, tiled=True)
    rows_in = both_recv[:, 0].reshape(slot_rows, model_width)
    grads_in = both_recv[:, 1].reshape(slot_rows, model_width)
    n_dp = lax.axis_size("dp")
    grid_x = 4 if n_dp % 4 == 0 else 1
    piece_in, piece_out = gather_weights(w_in[0], w_out[0], n_dp // grid_x, grid_x)
    pre = lax.dot_general(
        rows_in, piece_in, (((1,), (1,)), ((), ())), preferred_element_type=jnp.float32
    )
    acts = gelu_tanh(pre).astype(jnp.bfloat16)
    grad_act = lax.dot_general(
        grads_in, piece_out, (((1,), (1,)), ((), ())), preferred_element_type=jnp.float32
    )
    dpre = (grad_act * gelu_slope(pre)).astype(jnp.bfloat16)
    slot_sum = jnp.dot(dpre, piece_in, preferred_element_type=jnp.float32)
    slot_sum, acts_all, dpre_all = (slot_sum, acts, dpre)
    returned = lax.all_to_all(
        slot_sum.astype(jnp.bfloat16).reshape(experts, capacity, model_width),
        "expert",
        split_axis=0,
        concat_axis=0,
        tiled=True,
    )
    token_grads = lax.dot_general(
        route_mat,
        returned.reshape(slot_rows, model_width),
        (((0,), (0,)), ((), ())),
        preferred_element_type=jnp.float32,
    )
    d_tokens = token_grads.astype(jnp.bfloat16)
    term_in = lax.dot_general(
        dpre_all, rows_in, (((0,), (0,)), ((), ())), preferred_element_type=jnp.float32
    )
    term_out = lax.dot_general(
        acts_all, grads_in, (((0,), (0,)), ((), ())), preferred_element_type=jnp.float32
    )
    grad_in = lax.psum_scatter(term_in.astype(jnp.bfloat16), "dp", scatter_dimension=0, tiled=True)
    grad_in = grad_in.astype(jnp.float32)[None]
    parts_out = lax.all_to_all(
        term_out.astype(jnp.bfloat16).reshape(n_dp, shard_rows, model_width),
        "dp",
        split_axis=0,
        concat_axis=0,
        tiled=True,
    )
    grad_out = jnp.sum(parts_out.astype(jnp.float32), axis=0)[None]
    return (d_tokens, grad_in, grad_out)


def solution(mesh):
    in_specs = (
        P(("dp", "expert"), None),
        P(("dp", "expert"), None),
        P(("dp", "expert"), None),
        P(("dp", "expert"), None),
        P("expert", "dp", None),
        P("expert", "dp", None),
    )
    out_specs = (P(("dp", "expert"), None), P("expert", "dp", None), P("expert", "dp", None))
    return jax.shard_map(shards, mesh=mesh, in_specs=in_specs, out_specs=out_specs, check_vma=False)
```

```python
import jax
import jax.numpy as jnp
from jax import lax
from jax.sharding import PartitionSpec as P

tanh_coef = 0.7978845608028654
cubic_coef = 0.044715


def gelu_tanh(value):
    inner = tanh_coef * (value + cubic_coef * value * value * value)
    return 0.5 * value * (1.0 + jnp.tanh(inner))


def gelu_slope(value):
    inner = tanh_coef * (value + cubic_coef * value * value * value)
    slope_t = jnp.tanh(inner)
    return 0.5 * (1.0 + slope_t) + 0.5 * value * (1.0 - slope_t * slope_t) * tanh_coef * (
        1.0 + 3.0 * cubic_coef * value * value
    )


def dispatch_tables(route_blk, gate_blk, experts, capacity):
    tok_rows = route_blk.shape[0]
    flat = route_blk.reshape(-1)
    onehot = (flat[:, None] == jnp.arange(experts, dtype=jnp.int32)[None, :]).astype(jnp.int32)
    before = jnp.cumsum(onehot, axis=0) - onehot
    position = jnp.sum(before * onehot, axis=1)
    slots = (flat * capacity + position).reshape(tok_rows, -1)
    slot_ids = jnp.arange(experts * capacity, dtype=jnp.int32)
    placed = slot_ids[:, None, None] == slots[None, :, :]
    route_mat = jnp.sum(placed.astype(jnp.int32), axis=2).astype(jnp.bfloat16)
    gate_slot = jnp.sum(jnp.where(placed, gate_blk[None, :, :], jnp.float32(0.0)), axis=(1, 2))
    return (route_mat, gate_slot)


def grid_perm(ny, nx, dim, sign):
    pairs = []
    for d in range(ny * nx):
        cy, cx = divmod(d, nx)
        if dim == "x":
            pairs.append((d, cy * nx + (cx + sign) % nx))
        else:
            pairs.append((d, ((cy + sign) % ny) * nx + cx))
    return pairs


def ring_gather(piece, n, perm, sign):
    got = [None] * n
    got[0] = piece
    cur = piece
    for s in range(n - 1):
        cur = lax.ppermute(cur, "dp", perm)
        got[(sign * (s + 1)) % n] = cur
    return jnp.stack(got)


def grid_gather(piece, ny, nx, first, second):
    sizes = {"x": nx, "y": ny}
    g1 = ring_gather(piece, sizes[first[0]], grid_perm(ny, nx, *first), first[1])
    g2 = ring_gather(g1, sizes[second[0]], grid_perm(ny, nx, *second), second[1])
    if first[0] == "x":
        g2 = jnp.swapaxes(g2, 0, 1)
    return g2


def ring_reduce(blocks, n, perm, sign):
    acc = blocks[sign % n]
    for s in range(n - 1):
        recv = lax.ppermute(acc.astype(jnp.bfloat16), "dp", perm)
        acc = recv.astype(jnp.float32) + blocks[(sign * (s + 2)) % n]
    return acc


def grid_reduce(term, ny, nx, first, second):
    sizes = {"x": nx, "y": ny}
    n1, n2 = sizes[first[0]], sizes[second[0]]
    if first[0] == "x":
        blocks = [term[k] for k in range(n1)]
    else:
        blocks = [term[:, k] for k in range(n1)]
    part = ring_reduce(blocks, n1, grid_perm(ny, nx, *first), first[1])
    return ring_reduce([part[k] for k in range(n2)], n2, grid_perm(ny, nx, *second), second[1])


STREAMS = ((("x", 1), ("y", 1)), (("x", -1), ("y", -1)), (("y", 1), ("x", 1)), (("y", -1), ("x", -1)))


def shards(tokens, cotangent, routes, gates, w_in, w_out):
    experts = lax.axis_size("expert")
    tok_rows, model_width = tokens.shape
    top_count = routes.shape[1]
    capacity = 3 * tok_rows * top_count // experts
    shard_rows = w_in.shape[1]
    slot_rows = experts * capacity
    route_mat, gate_slot = dispatch_tables(routes, gates, experts, capacity)
    rows_sent = jnp.dot(route_mat, tokens, preferred_element_type=jnp.float32).astype(jnp.bfloat16)
    grad_rows = jnp.dot(route_mat, cotangent, preferred_element_type=jnp.float32)
    grads_sent = (gate_slot[:, None] * grad_rows).astype(jnp.bfloat16)
    both_sent = jnp.stack(
        [rows_sent.reshape(experts, capacity, model_width), grads_sent.reshape(experts, capacity, model_width)],
        axis=1,
    )
    both_recv = lax.all_to_all(both_sent, "expert", split_axis=0, concat_axis=0, tiled=True)
    rows_in = both_recv[:, 0].reshape(slot_rows, model_width)
    grads_in = both_recv[:, 1].reshape(slot_rows, model_width)
    n_dp = lax.axis_size("dp")
    nx = 4 if n_dp % 4 == 0 else 1
    ny = n_dp // nx
    half = shard_rows // 2
    halves = []
    for h in range(2):
        rows_h = slice(h * half, (h + 1) * half)
        in_h = grid_gather(w_in[0][rows_h], ny, nx, *STREAMS[h])
        out_h = grid_gather(w_out[0][rows_h], ny, nx, *STREAMS[2 + h])
        halves.append((in_h.reshape(-1, model_width), out_h.reshape(-1, model_width)))
    slot_sum = None
    terms = []
    for piece_in, piece_out in halves:
        pre = lax.dot_general(
            rows_in, piece_in, (((1,), (1,)), ((), ())), preferred_element_type=jnp.float32
        )
        acts = gelu_tanh(pre).astype(jnp.bfloat16)
        grad_act = lax.dot_general(
            grads_in, piece_out, (((1,), (1,)), ((), ())), preferred_element_type=jnp.float32
        )
        dpre = (grad_act * gelu_slope(pre)).astype(jnp.bfloat16)
        part = jnp.dot(dpre, piece_in, preferred_element_type=jnp.float32)
        slot_sum = part if slot_sum is None else slot_sum + part
        term_in = lax.dot_general(
            dpre, rows_in, (((0,), (0,)), ((), ())), preferred_element_type=jnp.float32
        )
        term_out = lax.dot_general(
            acts, grads_in, (((0,), (0,)), ((), ())), preferred_element_type=jnp.float32
        )
        terms.append((term_in, term_out))
    returned = lax.all_to_all(
        slot_sum.astype(jnp.bfloat16).reshape(experts, capacity, model_width),
        "expert",
        split_axis=0,
        concat_axis=0,
        tiled=True,
    )
    token_grads = lax.dot_general(
        route_mat,
        returned.reshape(slot_rows, model_width),
        (((0,), (0,)), ((), ())),
        preferred_element_type=jnp.float32,
    )
    d_tokens = token_grads.astype(jnp.bfloat16)
    grid_shape = (nx, ny, half, model_width)
    sums_in, sums_out = [], []
    for h in range(2):
        term_in = terms[h][0].astype(jnp.bfloat16).astype(jnp.float32).reshape(grid_shape)
        term_out = terms[h][1].astype(jnp.bfloat16).astype(jnp.float32).reshape(grid_shape)
        sums_in.append(grid_reduce(term_in, ny, nx, *STREAMS[h]))
        sums_out.append(grid_reduce(term_out, ny, nx, *STREAMS[2 + h]))
    grad_in = jnp.concatenate(sums_in, axis=0)[None]
    grad_out = jnp.concatenate(sums_out, axis=0)[None]
    return (d_tokens, grad_in, grad_out)


def solution(mesh):
    in_specs = (
        P(("dp", "expert"), None),
        P(("dp", "expert"), None),
        P(("dp", "expert"), None),
        P(("dp", "expert"), None),
        P("expert", "dp", None),
        P("expert", "dp", None),
    )
    out_specs = (P(("dp", "expert"), None), P("expert", "dp", None), P("expert", "dp", None))
    return jax.shard_map(shards, mesh=mesh, in_specs=in_specs, out_specs=out_specs, check_vma=False)
```

```python
import jax
import jax.numpy as jnp
from jax import lax
from jax.sharding import PartitionSpec as P

tanh_coef = 0.7978845608028654
cubic_coef = 0.044715


def gelu_tanh(value):
    inner = tanh_coef * (value + cubic_coef * value * value * value)
    return 0.5 * value * (1.0 + jnp.tanh(inner))


def gelu_slope(value):
    inner = tanh_coef * (value + cubic_coef * value * value * value)
    slope_t = jnp.tanh(inner)
    return 0.5 * (1.0 + slope_t) + 0.5 * value * (1.0 - slope_t * slope_t) * tanh_coef * (
        1.0 + 3.0 * cubic_coef * value * value
    )


def dispatch_tables(route_blk, gate_blk, experts, capacity):
    tok_rows = route_blk.shape[0]
    flat = route_blk.reshape(-1)
    onehot = (flat[:, None] == jnp.arange(experts, dtype=jnp.int32)[None, :]).astype(jnp.int32)
    before = jnp.cumsum(onehot, axis=0) - onehot
    position = jnp.sum(before * onehot, axis=1)
    slots = (flat * capacity + position).reshape(tok_rows, -1)
    slot_ids = jnp.arange(experts * capacity, dtype=jnp.int32)
    placed = slot_ids[:, None, None] == slots[None, :, :]
    route_mat = jnp.sum(placed.astype(jnp.int32), axis=2).astype(jnp.bfloat16)
    gate_slot = jnp.sum(jnp.where(placed, gate_blk[None, :, :], jnp.float32(0.0)), axis=(1, 2))
    return (route_mat, gate_slot)


def grid_perm(ny, nx, dim, sign):
    pairs = []
    for d in range(ny * nx):
        cy, cx = divmod(d, nx)
        if dim == "x":
            pairs.append((d, cy * nx + (cx + sign) % nx))
        else:
            pairs.append((d, ((cy + sign) % ny) * nx + cx))
    return pairs


def ring_gather(piece, n, perm, sign):
    got = [None] * n
    got[0] = piece
    cur = piece
    for s in range(n - 1):
        cur = lax.ppermute(cur, "dp", perm)
        got[(sign * (s + 1)) % n] = cur
    return jnp.stack(got)


def grid_gather(piece, ny, nx, first, second):
    sizes = {"x": nx, "y": ny}
    g1 = ring_gather(piece, sizes[first[0]], grid_perm(ny, nx, *first), first[1])
    g2 = ring_gather(g1, sizes[second[0]], grid_perm(ny, nx, *second), second[1])
    if first[0] == "x":
        g2 = jnp.swapaxes(g2, 0, 1)
    return g2


def ring_reduce(blocks, n, perm, sign):
    acc = blocks[sign % n]
    for s in range(n - 1):
        recv = lax.ppermute(acc.astype(jnp.bfloat16), "dp", perm)
        acc = recv.astype(jnp.float32) + blocks[(sign * (s + 2)) % n]
    return acc


def grid_reduce(term, ny, nx, first, second):
    sizes = {"x": nx, "y": ny}
    n1, n2 = sizes[first[0]], sizes[second[0]]
    if first[0] == "x":
        blocks = [term[k] for k in range(n1)]
    else:
        blocks = [term[:, k] for k in range(n1)]
    part = ring_reduce(blocks, n1, grid_perm(ny, nx, *first), first[1])
    return ring_reduce([part[k] for k in range(n2)], n2, grid_perm(ny, nx, *second), second[1])


STREAMS = ((("x", 1), ("y", 1)), (("x", -1), ("y", -1)), (("y", 1), ("x", 1)), (("y", -1), ("x", -1)))
GATHER_STREAMS = ((("x", 1), ("y", 1)), (("y", -1), ("x", -1)))


def relative_order(full, ny, nx):
    me = lax.axis_index("dp")
    cy, cx = me // nx, me % nx
    kx, ky = jnp.divmod(jnp.arange(ny * nx, dtype=jnp.int32), ny)
    index = ((cy - ky) % ny) * nx + (cx - kx) % nx
    return jnp.take(full.reshape(ny * nx, -1, full.shape[1]), index, axis=0)


def shards(tokens, cotangent, routes, gates, w_in, w_out):
    experts = lax.axis_size("expert")
    tok_rows, model_width = tokens.shape
    top_count = routes.shape[1]
    capacity = 3 * tok_rows * top_count // experts
    shard_rows = w_in.shape[1]
    slot_rows = experts * capacity
    route_mat, gate_slot = dispatch_tables(routes, gates, experts, capacity)
    rows_sent = jnp.dot(route_mat, tokens, preferred_element_type=jnp.float32).astype(jnp.bfloat16)
    grad_rows = jnp.dot(route_mat, cotangent, preferred_element_type=jnp.float32)
    grads_sent = (gate_slot[:, None] * grad_rows).astype(jnp.bfloat16)
    both_sent = jnp.stack(
        [rows_sent.reshape(experts, capacity, model_width), grads_sent.reshape(experts, capacity, model_width)],
        axis=1,
    )
    both_recv = lax.all_to_all(both_sent, "expert", split_axis=0, concat_axis=0, tiled=True)
    rows_in = both_recv[:, 0].reshape(slot_rows, model_width)
    grads_in = both_recv[:, 1].reshape(slot_rows, model_width)
    n_dp = lax.axis_size("dp")
    nx = 4 if n_dp % 4 == 0 else 1
    ny = n_dp // nx
    half = shard_rows // 2
    full_out = relative_order(lax.all_gather(w_out[0], "dp", axis=0, tiled=True), ny, nx)
    halves = []
    for h in range(2):
        rows_h = slice(h * half, (h + 1) * half)
        in_h = grid_gather(w_in[0][rows_h], ny, nx, *GATHER_STREAMS[h])
        out_h = full_out[:, rows_h]
        halves.append((in_h.reshape(-1, model_width), out_h.reshape(-1, model_width)))
    slot_sum = None
    terms = []
    for piece_in, piece_out in halves:
        pre = lax.dot_general(
            rows_in, piece_in, (((1,), (1,)), ((), ())), preferred_element_type=jnp.float32
        )
        acts = gelu_tanh(pre).astype(jnp.bfloat16)
        grad_act = lax.dot_general(
            grads_in, piece_out, (((1,), (1,)), ((), ())), preferred_element_type=jnp.float32
        )
        dpre = (grad_act * gelu_slope(pre)).astype(jnp.bfloat16)
        part = jnp.dot(dpre, piece_in, preferred_element_type=jnp.float32)
        slot_sum = part if slot_sum is None else slot_sum + part
        term_in = lax.dot_general(
            dpre, rows_in, (((0,), (0,)), ((), ())), preferred_element_type=jnp.float32
        )
        term_out = lax.dot_general(
            acts, grads_in, (((0,), (0,)), ((), ())), preferred_element_type=jnp.float32
        )
        terms.append((term_in, term_out))
    returned = lax.all_to_all(
        slot_sum.astype(jnp.bfloat16).reshape(experts, capacity, model_width),
        "expert",
        split_axis=0,
        concat_axis=0,
        tiled=True,
    )
    token_grads = lax.dot_general(
        route_mat,
        returned.reshape(slot_rows, model_width),
        (((0,), (0,)), ((), ())),
        preferred_element_type=jnp.float32,
    )
    d_tokens = token_grads.astype(jnp.bfloat16)
    grid_shape = (nx, ny, half, model_width)
    sums_in, sums_out = [], []
    for h in range(2):
        term_in = terms[h][0].astype(jnp.bfloat16).astype(jnp.float32).reshape(grid_shape)
        term_out = terms[h][1].astype(jnp.bfloat16).astype(jnp.float32).reshape(grid_shape)
        sums_in.append(grid_reduce(term_in, ny, nx, *STREAMS[h]))
        sums_out.append(grid_reduce(term_out, ny, nx, *STREAMS[2 + h]))
    grad_in = jnp.concatenate(sums_in, axis=0)[None]
    grad_out = jnp.concatenate(sums_out, axis=0)[None]
    return (d_tokens, grad_in, grad_out)


def solution(mesh):
    in_specs = (
        P(("dp", "expert"), None),
        P(("dp", "expert"), None),
        P(("dp", "expert"), None),
        P(("dp", "expert"), None),
        P("expert", "dp", None),
        P("expert", "dp", None),
    )
    out_specs = (P(("dp", "expert"), None), P("expert", "dp", None), P("expert", "dp", None))
    return jax.shard_map(shards, mesh=mesh, in_specs=in_specs, out_specs=out_specs, check_vma=False)
```

```python
import jax
import jax.numpy as jnp
from jax import lax
from jax.sharding import PartitionSpec as P

tanh_coef = 0.7978845608028654
cubic_coef = 0.044715


def gelu_tanh(value):
    inner = tanh_coef * (value + cubic_coef * value * value * value)
    return 0.5 * value * (1.0 + jnp.tanh(inner))


def gelu_slope(value):
    inner = tanh_coef * (value + cubic_coef * value * value * value)
    slope_t = jnp.tanh(inner)
    return 0.5 * (1.0 + slope_t) + 0.5 * value * (1.0 - slope_t * slope_t) * tanh_coef * (
        1.0 + 3.0 * cubic_coef * value * value
    )


def dispatch_tables(route_blk, gate_blk, experts, capacity):
    tok_rows = route_blk.shape[0]
    flat = route_blk.reshape(-1)
    onehot = (flat[:, None] == jnp.arange(experts, dtype=jnp.int32)[None, :]).astype(jnp.int32)
    before = jnp.cumsum(onehot, axis=0) - onehot
    position = jnp.sum(before * onehot, axis=1)
    slots = (flat * capacity + position).reshape(tok_rows, -1)
    slot_ids = jnp.arange(experts * capacity, dtype=jnp.int32)
    placed = slot_ids[:, None, None] == slots[None, :, :]
    route_mat = jnp.sum(placed.astype(jnp.int32), axis=2).astype(jnp.bfloat16)
    gate_slot = jnp.sum(jnp.where(placed, gate_blk[None, :, :], jnp.float32(0.0)), axis=(1, 2))
    return (route_mat, gate_slot)


def grid_perm(ny, nx, dim, sign):
    pairs = []
    for d in range(ny * nx):
        cy, cx = divmod(d, nx)
        if dim == "x":
            pairs.append((d, cy * nx + (cx + sign) % nx))
        else:
            pairs.append((d, ((cy + sign) % ny) * nx + cx))
    return pairs


def ring_gather(piece, n, perm, sign):
    got = [None] * n
    got[0] = piece
    cur = piece
    for s in range(n - 1):
        cur = lax.ppermute(cur, "dp", perm)
        got[(sign * (s + 1)) % n] = cur
    return jnp.stack(got)


def grid_gather(piece, ny, nx, first, second):
    sizes = {"x": nx, "y": ny}
    g1 = ring_gather(piece, sizes[first[0]], grid_perm(ny, nx, *first), first[1])
    g2 = ring_gather(g1, sizes[second[0]], grid_perm(ny, nx, *second), second[1])
    if first[0] == "x":
        g2 = jnp.swapaxes(g2, 0, 1)
    return g2


def ring_reduce(blocks, n, perm, sign):
    acc = blocks[sign % n]
    for s in range(n - 1):
        recv = lax.ppermute(acc.astype(jnp.bfloat16), "dp", perm)
        acc = recv.astype(jnp.float32) + blocks[(sign * (s + 2)) % n]
    return acc


def grid_reduce(term, ny, nx, first, second):
    sizes = {"x": nx, "y": ny}
    n1, n2 = sizes[first[0]], sizes[second[0]]
    if first[0] == "x":
        blocks = [term[k] for k in range(n1)]
    else:
        blocks = [term[:, k] for k in range(n1)]
    part = ring_reduce(blocks, n1, grid_perm(ny, nx, *first), first[1])
    return ring_reduce([part[k] for k in range(n2)], n2, grid_perm(ny, nx, *second), second[1])


STREAMS = ((("x", 1), ("y", 1)), (("x", -1), ("y", -1)), (("y", 1), ("x", 1)), (("y", -1), ("x", -1)))
GATHER_STREAMS = ((("x", 1), ("y", 1)), (("y", -1), ("x", -1)))


def relative_order(full, ny, nx):
    me = lax.axis_index("dp")
    cy, cx = me // nx, me % nx
    kx, ky = jnp.divmod(jnp.arange(ny * nx, dtype=jnp.int32), ny)
    index = ((cy - ky) % ny) * nx + (cx - kx) % nx
    return jnp.take(full.reshape(ny * nx, -1, full.shape[1]), index, axis=0)


def shards(tokens, cotangent, routes, gates, w_in, w_out):
    experts = lax.axis_size("expert")
    tok_rows, model_width = tokens.shape
    top_count = routes.shape[1]
    capacity = 3 * tok_rows * top_count // experts
    shard_rows = w_in.shape[1]
    slot_rows = experts * capacity
    route_mat, gate_slot = dispatch_tables(routes, gates, experts, capacity)
    rows_sent = jnp.dot(route_mat, tokens, preferred_element_type=jnp.float32).astype(jnp.bfloat16)
    grad_rows = jnp.dot(route_mat, cotangent, preferred_element_type=jnp.float32)
    grads_sent = (gate_slot[:, None] * grad_rows).astype(jnp.bfloat16)
    both_sent = jnp.stack(
        [rows_sent.reshape(experts, capacity, model_width), grads_sent.reshape(experts, capacity, model_width)],
        axis=1,
    )
    both_recv = lax.all_to_all(both_sent, "expert", split_axis=0, concat_axis=0, tiled=True)
    rows_in = both_recv[:, 0].reshape(slot_rows, model_width)
    grads_in = both_recv[:, 1].reshape(slot_rows, model_width)
    n_dp = lax.axis_size("dp")
    nx = 4 if n_dp % 4 == 0 else 1
    ny = n_dp // nx
    half = shard_rows // 2
    full_out = relative_order(lax.all_gather(w_out[0], "dp", axis=0, tiled=True), ny, nx)
    full_out, rows_in, grads_in = lax.optimization_barrier((full_out, rows_in, grads_in))
    halves = []
    for h in range(2):
        rows_h = slice(h * half, (h + 1) * half)
        in_h = grid_gather(w_in[0][rows_h], ny, nx, *GATHER_STREAMS[h])
        out_h = full_out[:, rows_h]
        halves.append((in_h.reshape(-1, model_width), out_h.reshape(-1, model_width)))
    slot_sum = None
    terms = []
    for piece_in, piece_out in halves:
        pre = lax.dot_general(
            rows_in, piece_in, (((1,), (1,)), ((), ())), preferred_element_type=jnp.float32
        )
        acts = gelu_tanh(pre).astype(jnp.bfloat16)
        grad_act = lax.dot_general(
            grads_in, piece_out, (((1,), (1,)), ((), ())), preferred_element_type=jnp.float32
        )
        dpre = (grad_act * gelu_slope(pre)).astype(jnp.bfloat16)
        part = jnp.dot(dpre, piece_in, preferred_element_type=jnp.float32)
        slot_sum = part if slot_sum is None else slot_sum + part
        term_in = lax.dot_general(
            dpre, rows_in, (((0,), (0,)), ((), ())), preferred_element_type=jnp.float32
        )
        term_out = lax.dot_general(
            acts, grads_in, (((0,), (0,)), ((), ())), preferred_element_type=jnp.float32
        )
        terms.append((term_in, term_out))
    returned = lax.all_to_all(
        slot_sum.astype(jnp.bfloat16).reshape(experts, capacity, model_width),
        "expert",
        split_axis=0,
        concat_axis=0,
        tiled=True,
    )
    token_grads = lax.dot_general(
        route_mat,
        returned.reshape(slot_rows, model_width),
        (((0,), (0,)), ((), ())),
        preferred_element_type=jnp.float32,
    )
    d_tokens = token_grads.astype(jnp.bfloat16)
    grid_shape = (nx, ny, half, model_width)
    sums_in, sums_out = [], []
    for h in range(2):
        term_in = terms[h][0].astype(jnp.bfloat16).astype(jnp.float32).reshape(grid_shape)
        term_out = terms[h][1].astype(jnp.bfloat16).astype(jnp.float32).reshape(grid_shape)
        sums_in.append(grid_reduce(term_in, ny, nx, *STREAMS[h]))
        sums_out.append(grid_reduce(term_out, ny, nx, *STREAMS[2 + h]))
    grad_in = jnp.concatenate(sums_in, axis=0)[None]
    grad_out = jnp.concatenate(sums_out, axis=0)[None]
    return (d_tokens, grad_in, grad_out)


def solution(mesh):
    in_specs = (
        P(("dp", "expert"), None),
        P(("dp", "expert"), None),
        P(("dp", "expert"), None),
        P(("dp", "expert"), None),
        P("expert", "dp", None),
        P("expert", "dp", None),
    )
    out_specs = (P(("dp", "expert"), None), P("expert", "dp", None), P("expert", "dp", None))
    return jax.shard_map(shards, mesh=mesh, in_specs=in_specs, out_specs=out_specs, check_vma=False)
```

```python
import jax
import jax.numpy as jnp
from jax import lax
from jax.sharding import PartitionSpec as P

tanh_coef = 0.7978845608028654
cubic_coef = 0.044715


def gelu_tanh(value):
    inner = tanh_coef * (value + cubic_coef * value * value * value)
    return 0.5 * value * (1.0 + jnp.tanh(inner))


def gelu_slope(value):
    inner = tanh_coef * (value + cubic_coef * value * value * value)
    slope_t = jnp.tanh(inner)
    return 0.5 * (1.0 + slope_t) + 0.5 * value * (1.0 - slope_t * slope_t) * tanh_coef * (
        1.0 + 3.0 * cubic_coef * value * value
    )


def dispatch_tables(route_blk, gate_blk, experts, capacity):
    tok_rows = route_blk.shape[0]
    flat = route_blk.reshape(-1)
    onehot = (flat[:, None] == jnp.arange(experts, dtype=jnp.int32)[None, :]).astype(jnp.int32)
    before = jnp.cumsum(onehot, axis=0) - onehot
    position = jnp.sum(before * onehot, axis=1)
    slots = (flat * capacity + position).reshape(tok_rows, -1)
    slot_ids = jnp.arange(experts * capacity, dtype=jnp.int32)
    placed = slot_ids[:, None, None] == slots[None, :, :]
    route_mat = jnp.sum(placed.astype(jnp.int32), axis=2).astype(jnp.bfloat16)
    gate_slot = jnp.sum(jnp.where(placed, gate_blk[None, :, :], jnp.float32(0.0)), axis=(1, 2))
    return (route_mat, gate_slot)


def grid_perm(ny, nx, dim, sign):
    pairs = []
    for d in range(ny * nx):
        cy, cx = divmod(d, nx)
        if dim == "x":
            pairs.append((d, cy * nx + (cx + sign) % nx))
        else:
            pairs.append((d, ((cy + sign) % ny) * nx + cx))
    return pairs


def ring_gather(piece, n, perm, sign):
    got = [None] * n
    got[0] = piece
    cur = piece
    for s in range(n - 1):
        cur = lax.ppermute(cur, "dp", perm)
        got[(sign * (s + 1)) % n] = cur
    return jnp.stack(got)


def grid_gather(piece, ny, nx, first, second):
    sizes = {"x": nx, "y": ny}
    g1 = ring_gather(piece, sizes[first[0]], grid_perm(ny, nx, *first), first[1])
    g2 = ring_gather(g1, sizes[second[0]], grid_perm(ny, nx, *second), second[1])
    if first[0] == "x":
        g2 = jnp.swapaxes(g2, 0, 1)
    return g2


def ring_reduce(blocks, n, perm, sign):
    acc = blocks[sign % n]
    for s in range(n - 1):
        recv = lax.ppermute(acc.astype(jnp.bfloat16), "dp", perm)
        acc = recv.astype(jnp.float32) + blocks[(sign * (s + 2)) % n]
    return acc


def grid_reduce(term, ny, nx, first, second):
    sizes = {"x": nx, "y": ny}
    n1, n2 = sizes[first[0]], sizes[second[0]]
    if first[0] == "x":
        blocks = [term[k] for k in range(n1)]
    else:
        blocks = [term[:, k] for k in range(n1)]
    part = ring_reduce(blocks, n1, grid_perm(ny, nx, *first), first[1])
    return ring_reduce([part[k] for k in range(n2)], n2, grid_perm(ny, nx, *second), second[1])


STREAMS = ((("x", 1), ("y", 1)), (("x", -1), ("y", -1)), (("y", 1), ("x", 1)), (("y", -1), ("x", -1)))


def shards(tokens, cotangent, routes, gates, w_in, w_out):
    experts = lax.axis_size("expert")
    tok_rows, model_width = tokens.shape
    top_count = routes.shape[1]
    capacity = 3 * tok_rows * top_count // experts
    shard_rows = w_in.shape[1]
    slot_rows = experts * capacity
    route_mat, gate_slot = dispatch_tables(routes, gates, experts, capacity)
    rows_sent = jnp.dot(route_mat, tokens, preferred_element_type=jnp.float32).astype(jnp.bfloat16)
    grad_rows = jnp.dot(route_mat, cotangent, preferred_element_type=jnp.float32)
    grads_sent = (gate_slot[:, None] * grad_rows).astype(jnp.bfloat16)
    both_sent = jnp.stack(
        [rows_sent.reshape(experts, capacity, model_width), grads_sent.reshape(experts, capacity, model_width)],
        axis=1,
    )
    both_recv = lax.all_to_all(both_sent, "expert", split_axis=0, concat_axis=0, tiled=True)
    rows_in = both_recv[:, 0].reshape(slot_rows, model_width)
    grads_in = both_recv[:, 1].reshape(slot_rows, model_width)
    n_dp = lax.axis_size("dp")
    nx = 4 if n_dp % 4 == 0 else 1
    ny = n_dp // nx
    half = shard_rows // 2
    halves = []
    for h in range(2):
        rows_h = slice(h * half, (h + 1) * half)
        own_in, own_out = w_in[0][rows_h], w_out[0][rows_h]
        if halves:
            own_in, own_out, rows_in, grads_in = lax.optimization_barrier(
                (own_in, own_out, rows_in, grads_in) + halves[-1]
            )[:4]
        in_h = grid_gather(own_in, ny, nx, *STREAMS[h])
        out_h = grid_gather(own_out, ny, nx, *STREAMS[2 + h])
        halves.append((in_h.reshape(-1, model_width), out_h.reshape(-1, model_width)))
    slot_sum = None
    terms = []
    for piece_in, piece_out in halves:
        pre = lax.dot_general(
            rows_in, piece_in, (((1,), (1,)), ((), ())), preferred_element_type=jnp.float32
        )
        acts = gelu_tanh(pre).astype(jnp.bfloat16)
        grad_act = lax.dot_general(
            grads_in, piece_out, (((1,), (1,)), ((), ())), preferred_element_type=jnp.float32
        )
        dpre = (grad_act * gelu_slope(pre)).astype(jnp.bfloat16)
        part = jnp.dot(dpre, piece_in, preferred_element_type=jnp.float32)
        slot_sum = part if slot_sum is None else slot_sum + part
        term_in = lax.dot_general(
            dpre, rows_in, (((0,), (0,)), ((), ())), preferred_element_type=jnp.float32
        )
        term_out = lax.dot_general(
            acts, grads_in, (((0,), (0,)), ((), ())), preferred_element_type=jnp.float32
        )
        terms.append((term_in, term_out))
    returned = lax.all_to_all(
        slot_sum.astype(jnp.bfloat16).reshape(experts, capacity, model_width),
        "expert",
        split_axis=0,
        concat_axis=0,
        tiled=True,
    )
    token_grads = lax.dot_general(
        route_mat,
        returned.reshape(slot_rows, model_width),
        (((0,), (0,)), ((), ())),
        preferred_element_type=jnp.float32,
    )
    d_tokens = token_grads.astype(jnp.bfloat16)
    grid_shape = (nx, ny, half, model_width)
    sums_in, sums_out = [], []
    for h in range(2):
        term_in = terms[h][0].astype(jnp.bfloat16).astype(jnp.float32).reshape(grid_shape)
        term_out = terms[h][1].astype(jnp.bfloat16).astype(jnp.float32).reshape(grid_shape)
        sums_in.append(grid_reduce(term_in, ny, nx, *STREAMS[h]))
        sums_out.append(grid_reduce(term_out, ny, nx, *STREAMS[2 + h]))
    grad_in = jnp.concatenate(sums_in, axis=0)[None]
    grad_out = jnp.concatenate(sums_out, axis=0)[None]
    return (d_tokens, grad_in, grad_out)


def solution(mesh):
    in_specs = (
        P(("dp", "expert"), None),
        P(("dp", "expert"), None),
        P(("dp", "expert"), None),
        P(("dp", "expert"), None),
        P("expert", "dp", None),
        P("expert", "dp", None),
    )
    out_specs = (P(("dp", "expert"), None), P("expert", "dp", None), P("expert", "dp", None))
    return jax.shard_map(shards, mesh=mesh, in_specs=in_specs, out_specs=out_specs, check_vma=False)
```

```python
import jax
import jax.numpy as jnp
from jax import lax
from jax.sharding import PartitionSpec as P

tanh_coef = 0.7978845608028654
cubic_coef = 0.044715


def gelu_tanh(value):
    inner = tanh_coef * (value + cubic_coef * value * value * value)
    return 0.5 * value * (1.0 + jnp.tanh(inner))


def gelu_slope(value):
    inner = tanh_coef * (value + cubic_coef * value * value * value)
    slope_t = jnp.tanh(inner)
    return 0.5 * (1.0 + slope_t) + 0.5 * value * (1.0 - slope_t * slope_t) * tanh_coef * (
        1.0 + 3.0 * cubic_coef * value * value
    )


def dispatch_tables(route_blk, gate_blk, experts, capacity):
    tok_rows = route_blk.shape[0]
    flat = route_blk.reshape(-1)
    onehot = (flat[:, None] == jnp.arange(experts, dtype=jnp.int32)[None, :]).astype(jnp.int32)
    before = jnp.cumsum(onehot, axis=0) - onehot
    position = jnp.sum(before * onehot, axis=1)
    slots = (flat * capacity + position).reshape(tok_rows, -1)
    slot_ids = jnp.arange(experts * capacity, dtype=jnp.int32)
    placed = slot_ids[:, None, None] == slots[None, :, :]
    route_mat = jnp.sum(placed.astype(jnp.int32), axis=2).astype(jnp.bfloat16)
    gate_slot = jnp.sum(jnp.where(placed, gate_blk[None, :, :], jnp.float32(0.0)), axis=(1, 2))
    return (route_mat, gate_slot)


def grid_perm(ny, nx, dim, sign):
    pairs = []
    for d in range(ny * nx):
        cy, cx = divmod(d, nx)
        if dim == "x":
            pairs.append((d, cy * nx + (cx + sign) % nx))
        else:
            pairs.append((d, ((cy + sign) % ny) * nx + cx))
    return pairs


def ring_gather(piece, n, perm, sign):
    got = [None] * n
    got[0] = piece
    cur = piece
    for s in range(n - 1):
        cur = lax.ppermute(cur, "dp", perm)
        got[(sign * (s + 1)) % n] = cur
    return jnp.stack(got)


def grid_gather(piece, ny, nx, first, second):
    sizes = {"x": nx, "y": ny}
    g1 = ring_gather(piece, sizes[first[0]], grid_perm(ny, nx, *first), first[1])
    g2 = ring_gather(g1, sizes[second[0]], grid_perm(ny, nx, *second), second[1])
    if first[0] == "x":
        g2 = jnp.swapaxes(g2, 0, 1)
    return g2


def ring_reduce(blocks, n, perm, sign):
    acc = blocks[sign % n]
    for s in range(n - 1):
        recv = lax.ppermute(acc.astype(jnp.bfloat16), "dp", perm)
        acc = recv.astype(jnp.float32) + blocks[(sign * (s + 2)) % n]
    return acc


def grid_reduce(term, ny, nx, first, second):
    sizes = {"x": nx, "y": ny}
    n1, n2 = sizes[first[0]], sizes[second[0]]
    if first[0] == "x":
        blocks = [term[k] for k in range(n1)]
    else:
        blocks = [term[:, k] for k in range(n1)]
    part = ring_reduce(blocks, n1, grid_perm(ny, nx, *first), first[1])
    return ring_reduce([part[k] for k in range(n2)], n2, grid_perm(ny, nx, *second), second[1])


STREAMS = ((("x", 1), ("y", 1)), (("x", -1), ("y", -1)), (("y", 1), ("x", 1)), (("y", -1), ("x", -1)))


def shards(tokens, cotangent, routes, gates, w_in, w_out):
    experts = lax.axis_size("expert")
    tok_rows, model_width = tokens.shape
    top_count = routes.shape[1]
    capacity = 3 * tok_rows * top_count // experts
    shard_rows = w_in.shape[1]
    slot_rows = experts * capacity
    route_mat, gate_slot = dispatch_tables(routes, gates, experts, capacity)
    rows_sent = jnp.dot(route_mat, tokens, preferred_element_type=jnp.float32).astype(jnp.bfloat16)
    grad_rows = jnp.dot(route_mat, cotangent, preferred_element_type=jnp.float32)
    grads_sent = (gate_slot[:, None] * grad_rows).astype(jnp.bfloat16)
    both_sent = jnp.stack(
        [rows_sent.reshape(experts, capacity, model_width), grads_sent.reshape(experts, capacity, model_width)],
        axis=1,
    )
    both_recv = lax.all_to_all(both_sent, "expert", split_axis=0, concat_axis=0, tiled=True)
    rows_in = both_recv[:, 0].reshape(slot_rows, model_width)
    grads_in = both_recv[:, 1].reshape(slot_rows, model_width)
    n_dp = lax.axis_size("dp")
    nx = 4 if n_dp % 4 == 0 else 1
    ny = n_dp // nx
    cut = (shard_rows // 2) // 16 * 16 or shard_rows // 2
    cuts = (0, cut, shard_rows)
    halves = []
    for h in range(2):
        rows_h = slice(cuts[h], cuts[h + 1])
        in_h = grid_gather(w_in[0][rows_h], ny, nx, *STREAMS[h])
        out_h = grid_gather(w_out[0][rows_h], ny, nx, *STREAMS[2 + h])
        halves.append((in_h.reshape(-1, model_width), out_h.reshape(-1, model_width)))
    slot_sum = None
    terms = []
    for piece_in, piece_out in halves:
        pre = lax.dot_general(
            rows_in, piece_in, (((1,), (1,)), ((), ())), preferred_element_type=jnp.float32
        )
        acts = gelu_tanh(pre).astype(jnp.bfloat16)
        grad_act = lax.dot_general(
            grads_in, piece_out, (((1,), (1,)), ((), ())), preferred_element_type=jnp.float32
        )
        dpre = (grad_act * gelu_slope(pre)).astype(jnp.bfloat16)
        part = jnp.dot(dpre, piece_in, preferred_element_type=jnp.float32)
        slot_sum = part if slot_sum is None else slot_sum + part
        term_in = lax.dot_general(
            dpre, rows_in, (((0,), (0,)), ((), ())), preferred_element_type=jnp.float32
        )
        term_out = lax.dot_general(
            acts, grads_in, (((0,), (0,)), ((), ())), preferred_element_type=jnp.float32
        )
        terms.append((term_in, term_out))
    returned = lax.all_to_all(
        slot_sum.astype(jnp.bfloat16).reshape(experts, capacity, model_width),
        "expert",
        split_axis=0,
        concat_axis=0,
        tiled=True,
    )
    token_grads = lax.dot_general(
        route_mat,
        returned.reshape(slot_rows, model_width),
        (((0,), (0,)), ((), ())),
        preferred_element_type=jnp.float32,
    )
    d_tokens = token_grads.astype(jnp.bfloat16)
    sums_in, sums_out = [], []
    for h in range(2):
        grid_shape = (nx, ny, cuts[h + 1] - cuts[h], model_width)
        term_in = terms[h][0].astype(jnp.bfloat16).astype(jnp.float32).reshape(grid_shape)
        term_out = terms[h][1].astype(jnp.bfloat16).astype(jnp.float32).reshape(grid_shape)
        sums_in.append(grid_reduce(term_in, ny, nx, *STREAMS[h]))
        sums_out.append(grid_reduce(term_out, ny, nx, *STREAMS[2 + h]))
    grad_in = jnp.concatenate(sums_in, axis=0)[None]
    grad_out = jnp.concatenate(sums_out, axis=0)[None]
    return (d_tokens, grad_in, grad_out)


def solution(mesh):
    in_specs = (
        P(("dp", "expert"), None),
        P(("dp", "expert"), None),
        P(("dp", "expert"), None),
        P(("dp", "expert"), None),
        P("expert", "dp", None),
        P("expert", "dp", None),
    )
    out_specs = (P(("dp", "expert"), None), P("expert", "dp", None), P("expert", "dp", None))
    return jax.shard_map(shards, mesh=mesh, in_specs=in_specs, out_specs=out_specs, check_vma=False)
```

```python
import jax
import jax.numpy as jnp
from jax import lax
from jax.sharding import PartitionSpec as P

tanh_coef = 0.7978845608028654
cubic_coef = 0.044715


def gelu_tanh(value):
    inner = tanh_coef * (value + cubic_coef * value * value * value)
    return 0.5 * value * (1.0 + jnp.tanh(inner))


def gelu_slope(value):
    inner = tanh_coef * (value + cubic_coef * value * value * value)
    slope_t = jnp.tanh(inner)
    return 0.5 * (1.0 + slope_t) + 0.5 * value * (1.0 - slope_t * slope_t) * tanh_coef * (
        1.0 + 3.0 * cubic_coef * value * value
    )


def dispatch_tables(route_blk, gate_blk, experts, capacity):
    tok_rows = route_blk.shape[0]
    flat = route_blk.reshape(-1)
    onehot = (flat[:, None] == jnp.arange(experts, dtype=jnp.int32)[None, :]).astype(jnp.int32)
    before = jnp.cumsum(onehot, axis=0) - onehot
    position = jnp.sum(before * onehot, axis=1)
    slots = (flat * capacity + position).reshape(tok_rows, -1)
    slot_ids = jnp.arange(experts * capacity, dtype=jnp.int32)
    placed = slot_ids[:, None, None] == slots[None, :, :]
    route_mat = jnp.sum(placed.astype(jnp.int32), axis=2).astype(jnp.bfloat16)
    gate_slot = jnp.sum(jnp.where(placed, gate_blk[None, :, :], jnp.float32(0.0)), axis=(1, 2))
    return (route_mat, gate_slot)


def grid_perm(ny, nx, dim, sign):
    pairs = []
    for d in range(ny * nx):
        cy, cx = divmod(d, nx)
        if dim == "x":
            pairs.append((d, cy * nx + (cx + sign) % nx))
        else:
            pairs.append((d, ((cy + sign) % ny) * nx + cx))
    return pairs


def ring_gather(piece, n, perm, sign):
    got = [None] * n
    got[0] = piece
    cur = piece
    for s in range(n - 1):
        cur = lax.ppermute(cur, "dp", perm)
        got[(sign * (s + 1)) % n] = cur
    return jnp.stack(got)


def loop_gather(pieces, n, perms, signs):
    bufs = tuple(jnp.zeros((n,) + p.shape, p.dtype).at[0].set(p) for p in pieces)

    def step(s, carry):
        curs, bufs = carry
        curs = tuple(lax.ppermute(c, "dp", pm) for c, pm in zip(curs, perms))
        bufs = tuple(
            lax.dynamic_update_index_in_dim(b, c, (sg * (s + 1)) % n, 0)
            for b, c, sg in zip(bufs, curs, signs)
        )
        return curs, bufs

    return lax.fori_loop(0, n - 1, step, (tuple(pieces), bufs))[1]


def loop_reduce(terms, axes, n, perms, signs):
    accs = tuple(lax.index_in_dim(t, sg % n, a, keepdims=False) for t, a, sg in zip(terms, axes, signs))

    def step(s, accs):
        recvs = tuple(lax.ppermute(a.astype(jnp.bfloat16), "dp", pm) for a, pm in zip(accs, perms))
        return tuple(
            r.astype(jnp.float32) + lax.dynamic_index_in_dim(t, (sg * (s + 2)) % n, ax, keepdims=False)
            for r, t, ax, sg in zip(recvs, terms, axes, signs)
        )

    return lax.fori_loop(0, n - 1, step, accs)


STREAMS = ((("x", 1), ("y", 1)), (("x", -1), ("y", -1)), (("y", 1), ("x", 1)), (("y", -1), ("x", -1)))


def all_gathers(pieces, ny, nx):
    assert nx == ny
    first = [grid_perm(ny, nx, *st[0]) for st in STREAMS]
    second = [grid_perm(ny, nx, *st[1]) for st in STREAMS]
    signs1 = [st[0][1] for st in STREAMS]
    signs2 = [st[1][1] for st in STREAMS]
    g1 = loop_gather(pieces, nx, first, signs1)
    g2 = loop_gather(g1, nx, second, signs2)
    return tuple(jnp.swapaxes(g, 0, 1) if st[0][0] == "x" else g for g, st in zip(g2, STREAMS))


def reduce_scatters(terms, ny, nx):
    assert nx == ny
    first = [grid_perm(ny, nx, *st[0]) for st in STREAMS]
    second = [grid_perm(ny, nx, *st[1]) for st in STREAMS]
    signs1 = [st[0][1] for st in STREAMS]
    signs2 = [st[1][1] for st in STREAMS]
    axes1 = [0 if st[0][0] == "x" else 1 for st in STREAMS]
    parts = loop_reduce(terms, axes1, nx, first, signs1)
    return loop_reduce(parts, [0] * len(terms), nx, second, signs2)


def shards(tokens, cotangent, routes, gates, w_in, w_out):
    experts = lax.axis_size("expert")
    tok_rows, model_width = tokens.shape
    top_count = routes.shape[1]
    capacity = 3 * tok_rows * top_count // experts
    shard_rows = w_in.shape[1]
    slot_rows = experts * capacity
    route_mat, gate_slot = dispatch_tables(routes, gates, experts, capacity)
    rows_sent = jnp.dot(route_mat, tokens, preferred_element_type=jnp.float32).astype(jnp.bfloat16)
    grad_rows = jnp.dot(route_mat, cotangent, preferred_element_type=jnp.float32)
    grads_sent = (gate_slot[:, None] * grad_rows).astype(jnp.bfloat16)
    both_sent = jnp.stack(
        [rows_sent.reshape(experts, capacity, model_width), grads_sent.reshape(experts, capacity, model_width)],
        axis=1,
    )
    both_recv = lax.all_to_all(both_sent, "expert", split_axis=0, concat_axis=0, tiled=True)
    rows_in = both_recv[:, 0].reshape(slot_rows, model_width)
    grads_in = both_recv[:, 1].reshape(slot_rows, model_width)
    n_dp = lax.axis_size("dp")
    nx = 4 if n_dp % 4 == 0 else 1
    ny = n_dp // nx
    half = shard_rows // 2
    in_a, in_b, out_a, out_b = all_gathers(
        (w_in[0][:half], w_in[0][half:], w_out[0][:half], w_out[0][half:]), ny, nx
    )
    halves = [
        (in_a.reshape(-1, model_width), out_a.reshape(-1, model_width)),
        (in_b.reshape(-1, model_width), out_b.reshape(-1, model_width)),
    ]
    slot_sum = None
    terms = []
    for piece_in, piece_out in halves:
        pre = lax.dot_general(
            rows_in, piece_in, (((1,), (1,)), ((), ())), preferred_element_type=jnp.float32
        )
        acts = gelu_tanh(pre).astype(jnp.bfloat16)
        grad_act = lax.dot_general(
            grads_in, piece_out, (((1,), (1,)), ((), ())), preferred_element_type=jnp.float32
        )
        dpre = (grad_act * gelu_slope(pre)).astype(jnp.bfloat16)
        part = jnp.dot(dpre, piece_in, preferred_element_type=jnp.float32)
        slot_sum = part if slot_sum is None else slot_sum + part
        term_in = lax.dot_general(
            dpre, rows_in, (((0,), (0,)), ((), ())), preferred_element_type=jnp.float32
        )
        term_out = lax.dot_general(
            acts, grads_in, (((0,), (0,)), ((), ())), preferred_element_type=jnp.float32
        )
        terms.append((term_in, term_out))
    returned = lax.all_to_all(
        slot_sum.astype(jnp.bfloat16).reshape(experts, capacity, model_width),
        "expert",
        split_axis=0,
        concat_axis=0,
        tiled=True,
    )
    token_grads = lax.dot_general(
        route_mat,
        returned.reshape(slot_rows, model_width),
        (((0,), (0,)), ((), ())),
        preferred_element_type=jnp.float32,
    )
    d_tokens = token_grads.astype(jnp.bfloat16)
    grid_shape = (nx, ny, half, model_width)
    rounded = [t.astype(jnp.bfloat16).astype(jnp.float32).reshape(grid_shape) for pair in terms for t in pair]
    in_a, in_b, out_a, out_b = reduce_scatters((rounded[0], rounded[2], rounded[1], rounded[3]), ny, nx)
    grad_in = jnp.concatenate([in_a, in_b], axis=0)[None]
    grad_out = jnp.concatenate([out_a, out_b], axis=0)[None]
    return (d_tokens, grad_in, grad_out)


def solution(mesh):
    in_specs = (
        P(("dp", "expert"), None),
        P(("dp", "expert"), None),
        P(("dp", "expert"), None),
        P(("dp", "expert"), None),
        P("expert", "dp", None),
        P("expert", "dp", None),
    )
    out_specs = (P(("dp", "expert"), None), P("expert", "dp", None), P("expert", "dp", None))
    return jax.shard_map(shards, mesh=mesh, in_specs=in_specs, out_specs=out_specs, check_vma=False)
```

```python
import jax
import jax.numpy as jnp
from jax import lax
from jax.sharding import PartitionSpec as P

tanh_coef = 0.7978845608028654
cubic_coef = 0.044715


def gelu_tanh(value):
    inner = tanh_coef * (value + cubic_coef * value * value * value)
    return 0.5 * value * (1.0 + jnp.tanh(inner))


def gelu_slope(value):
    inner = tanh_coef * (value + cubic_coef * value * value * value)
    slope_t = jnp.tanh(inner)
    return 0.5 * (1.0 + slope_t) + 0.5 * value * (1.0 - slope_t * slope_t) * tanh_coef * (
        1.0 + 3.0 * cubic_coef * value * value
    )


def dispatch_tables(route_blk, gate_blk, experts, capacity):
    tok_rows = route_blk.shape[0]
    flat = route_blk.reshape(-1)
    onehot = (flat[:, None] == jnp.arange(experts, dtype=jnp.int32)[None, :]).astype(jnp.int32)
    before = jnp.cumsum(onehot, axis=0) - onehot
    position = jnp.sum(before * onehot, axis=1)
    slots = (flat * capacity + position).reshape(tok_rows, -1)
    slot_ids = jnp.arange(experts * capacity, dtype=jnp.int32)
    placed = slot_ids[:, None, None] == slots[None, :, :]
    route_mat = jnp.sum(placed.astype(jnp.int32), axis=2).astype(jnp.bfloat16)
    gate_slot = jnp.sum(jnp.where(placed, gate_blk[None, :, :], jnp.float32(0.0)), axis=(1, 2))
    return (route_mat, gate_slot)


def grid_perm(ny, nx, dim, sign):
    pairs = []
    for d in range(ny * nx):
        cy, cx = divmod(d, nx)
        if dim == "x":
            pairs.append((d, cy * nx + (cx + sign) % nx))
        else:
            pairs.append((d, ((cy + sign) % ny) * nx + cx))
    return pairs


def ring_gather(piece, n, perm, sign):
    got = [None] * n
    got[0] = piece
    cur = piece
    for s in range(n - 1):
        cur = lax.ppermute(cur, "dp", perm)
        got[(sign * (s + 1)) % n] = cur
    return jnp.stack(got)


def grid_gather(piece, ny, nx, first, second):
    sizes = {"x": nx, "y": ny}
    g1 = ring_gather(piece, sizes[first[0]], grid_perm(ny, nx, *first), first[1])
    g2 = ring_gather(g1, sizes[second[0]], grid_perm(ny, nx, *second), second[1])
    if first[0] == "x":
        g2 = jnp.swapaxes(g2, 0, 1)
    return g2


def ring_reduce(blocks, n, perm, sign):
    acc = blocks[sign % n]
    for s in range(n - 1):
        recv = lax.ppermute(acc.astype(jnp.bfloat16), "dp", perm)
        acc = recv.astype(jnp.float32) + blocks[(sign * (s + 2)) % n].astype(jnp.float32)
    return acc


def grid_reduce(term, ny, nx, first, second):
    sizes = {"x": nx, "y": ny}
    n1, n2 = sizes[first[0]], sizes[second[0]]
    if first[0] == "x":
        blocks = [term[k] for k in range(n1)]
    else:
        blocks = [term[:, k] for k in range(n1)]
    part = ring_reduce(blocks, n1, grid_perm(ny, nx, *first), first[1])
    return ring_reduce([part[k] for k in range(n2)], n2, grid_perm(ny, nx, *second), second[1])


STREAMS = ((("x", 1), ("y", 1)), (("x", -1), ("y", -1)), (("y", 1), ("x", 1)), (("y", -1), ("x", -1)))


def shards(tokens, cotangent, routes, gates, w_in, w_out):
    experts = lax.axis_size("expert")
    tok_rows, model_width = tokens.shape
    top_count = routes.shape[1]
    capacity = 3 * tok_rows * top_count // experts
    shard_rows = w_in.shape[1]
    slot_rows = experts * capacity
    route_mat, gate_slot = dispatch_tables(routes, gates, experts, capacity)
    rows_sent = jnp.dot(route_mat, tokens, preferred_element_type=jnp.float32).astype(jnp.bfloat16)
    grad_rows = jnp.dot(route_mat, cotangent, preferred_element_type=jnp.float32)
    grads_sent = (gate_slot[:, None] * grad_rows).astype(jnp.bfloat16)
    both_sent = jnp.stack(
        [rows_sent.reshape(experts, capacity, model_width), grads_sent.reshape(experts, capacity, model_width)],
        axis=1,
    )
    both_recv = lax.all_to_all(both_sent, "expert", split_axis=0, concat_axis=0, tiled=True)
    rows_in = both_recv[:, 0].reshape(slot_rows, model_width)
    grads_in = both_recv[:, 1].reshape(slot_rows, model_width)
    n_dp = lax.axis_size("dp")
    nx = 4 if n_dp % 4 == 0 else 1
    ny = n_dp // nx
    half = shard_rows // 2
    halves = []
    for h in range(2):
        rows_h = slice(h * half, (h + 1) * half)
        in_h = grid_gather(w_in[0][rows_h], ny, nx, *STREAMS[h])
        out_h = grid_gather(w_out[0][rows_h], ny, nx, *STREAMS[2 + h])
        halves.append((in_h.reshape(-1, model_width), out_h.reshape(-1, model_width)))
    slot_sum = None
    terms = []
    for piece_in, piece_out in halves:
        pre = lax.dot_general(
            rows_in, piece_in, (((1,), (1,)), ((), ())), preferred_element_type=jnp.float32
        )
        acts = gelu_tanh(pre).astype(jnp.bfloat16)
        grad_act = lax.dot_general(
            grads_in, piece_out, (((1,), (1,)), ((), ())), preferred_element_type=jnp.float32
        )
        dpre = (grad_act * gelu_slope(pre)).astype(jnp.bfloat16)
        part = jnp.dot(dpre, piece_in, preferred_element_type=jnp.float32)
        slot_sum = part if slot_sum is None else slot_sum + part
        term_in = lax.dot_general(
            dpre, rows_in, (((0,), (0,)), ((), ())), preferred_element_type=jnp.float32
        )
        term_out = lax.dot_general(
            acts, grads_in, (((0,), (0,)), ((), ())), preferred_element_type=jnp.float32
        )
        terms.append((term_in, term_out))
    returned = lax.all_to_all(
        slot_sum.astype(jnp.bfloat16).reshape(experts, capacity, model_width),
        "expert",
        split_axis=0,
        concat_axis=0,
        tiled=True,
    )
    token_grads = lax.dot_general(
        route_mat,
        returned.reshape(slot_rows, model_width),
        (((0,), (0,)), ((), ())),
        preferred_element_type=jnp.float32,
    )
    d_tokens = token_grads.astype(jnp.bfloat16)
    grid_shape = (nx, ny, half, model_width)
    sums_in, sums_out = [], []
    for h in range(2):
        term_in = terms[h][0].astype(jnp.bfloat16).reshape(grid_shape)
        term_out = terms[h][1].astype(jnp.bfloat16).reshape(grid_shape)
        sums_in.append(grid_reduce(term_in, ny, nx, *STREAMS[h]))
        sums_out.append(grid_reduce(term_out, ny, nx, *STREAMS[2 + h]))
    grad_in = jnp.concatenate(sums_in, axis=0)[None]
    grad_out = jnp.concatenate(sums_out, axis=0)[None]
    return (d_tokens, grad_in, grad_out)


def solution(mesh):
    in_specs = (
        P(("dp", "expert"), None),
        P(("dp", "expert"), None),
        P(("dp", "expert"), None),
        P(("dp", "expert"), None),
        P("expert", "dp", None),
        P("expert", "dp", None),
    )
    out_specs = (P(("dp", "expert"), None), P("expert", "dp", None), P("expert", "dp", None))
    return jax.shard_map(shards, mesh=mesh, in_specs=in_specs, out_specs=out_specs, check_vma=False)
```

```python
import jax
import jax.numpy as jnp
from jax import lax
from jax.sharding import PartitionSpec as P

tanh_coef = 0.7978845608028654
cubic_coef = 0.044715


def gelu_tanh(value):
    inner = tanh_coef * (value + cubic_coef * value * value * value)
    return 0.5 * value * (1.0 + jnp.tanh(inner))


def gelu_slope(value):
    inner = tanh_coef * (value + cubic_coef * value * value * value)
    slope_t = jnp.tanh(inner)
    return 0.5 * (1.0 + slope_t) + 0.5 * value * (1.0 - slope_t * slope_t) * tanh_coef * (
        1.0 + 3.0 * cubic_coef * value * value
    )


def dispatch_tables(route_blk, gate_blk, experts, capacity):
    tok_rows = route_blk.shape[0]
    flat = route_blk.reshape(-1)
    onehot = (flat[:, None] == jnp.arange(experts, dtype=jnp.int32)[None, :]).astype(jnp.int32)
    before = jnp.cumsum(onehot, axis=0) - onehot
    position = jnp.sum(before * onehot, axis=1)
    slots = (flat * capacity + position).reshape(tok_rows, -1)
    slot_ids = jnp.arange(experts * capacity, dtype=jnp.int32)
    placed = slot_ids[:, None, None] == slots[None, :, :]
    route_mat = jnp.sum(placed.astype(jnp.int32), axis=2).astype(jnp.bfloat16)
    gate_slot = jnp.sum(jnp.where(placed, gate_blk[None, :, :], jnp.float32(0.0)), axis=(1, 2))
    return (route_mat, gate_slot)


def grid_perm(ny, nx, dim, sign):
    pairs = []
    for d in range(ny * nx):
        cy, cx = divmod(d, nx)
        if dim == "x":
            pairs.append((d, cy * nx + (cx + sign) % nx))
        else:
            pairs.append((d, ((cy + sign) % ny) * nx + cx))
    return pairs


def ring_gather(piece, n, perm, sign):
    got = [None] * n
    got[0] = piece
    cur = piece
    for s in range(n - 1):
        cur = lax.ppermute(cur, "dp", perm)
        got[(sign * (s + 1)) % n] = cur
    return jnp.stack(got)


def grid_gather(piece, ny, nx, first, second):
    sizes = {"x": nx, "y": ny}
    g1 = ring_gather(piece, sizes[first[0]], grid_perm(ny, nx, *first), first[1])
    g2 = ring_gather(g1, sizes[second[0]], grid_perm(ny, nx, *second), second[1])
    if first[0] == "x":
        g2 = jnp.swapaxes(g2, 0, 1)
    return g2


def ring_reduce(blocks, n, perm, sign):
    acc = blocks[sign % n]
    for s in range(n - 1):
        recv = lax.ppermute(acc.astype(jnp.bfloat16), "dp", perm)
        acc = recv.astype(jnp.float32) + blocks[(sign * (s + 2)) % n].astype(jnp.float32)
    return acc


def grid_reduce(term, ny, nx, first, second, companion=None):
    sizes = {"x": nx, "y": ny}
    n1, n2 = sizes[first[0]], sizes[second[0]]
    if first[0] == "x":
        blocks = [term[k] for k in range(n1)]
    else:
        blocks = [term[:, k] for k in range(n1)]
    part = ring_reduce(blocks, n1, grid_perm(ny, nx, *first), first[1])
    if companion is not None:
        part, companion = lax.optimization_barrier((part, companion))
    total = ring_reduce([part[k] for k in range(n2)], n2, grid_perm(ny, nx, *second), second[1])
    return total, companion


STREAMS = ((("x", 1), ("y", 1)), (("x", -1), ("y", -1)), (("y", 1), ("x", 1)), (("y", -1), ("x", -1)))


def shards(tokens, cotangent, routes, gates, w_in, w_out):
    experts = lax.axis_size("expert")
    tok_rows, model_width = tokens.shape
    top_count = routes.shape[1]
    capacity = 3 * tok_rows * top_count // experts
    shard_rows = w_in.shape[1]
    slot_rows = experts * capacity
    route_mat, gate_slot = dispatch_tables(routes, gates, experts, capacity)
    rows_sent = jnp.dot(route_mat, tokens, preferred_element_type=jnp.float32).astype(jnp.bfloat16)
    grad_rows = jnp.dot(route_mat, cotangent, preferred_element_type=jnp.float32)
    grads_sent = (gate_slot[:, None] * grad_rows).astype(jnp.bfloat16)
    both_sent = jnp.stack(
        [rows_sent.reshape(experts, capacity, model_width), grads_sent.reshape(experts, capacity, model_width)],
        axis=1,
    )
    both_recv = lax.all_to_all(both_sent, "expert", split_axis=0, concat_axis=0, tiled=True)
    rows_in = both_recv[:, 0].reshape(slot_rows, model_width)
    grads_in = both_recv[:, 1].reshape(slot_rows, model_width)
    n_dp = lax.axis_size("dp")
    nx = 4 if n_dp % 4 == 0 else 1
    ny = n_dp // nx
    half = shard_rows // 2
    halves = []
    for h in range(2):
        rows_h = slice(h * half, (h + 1) * half)
        in_h = grid_gather(w_in[0][rows_h], ny, nx, *STREAMS[h])
        out_h = grid_gather(w_out[0][rows_h], ny, nx, *STREAMS[2 + h])
        halves.append((in_h.reshape(-1, model_width), out_h.reshape(-1, model_width)))
    slot_sum = None
    terms = []
    for piece_in, piece_out in halves:
        pre = lax.dot_general(
            rows_in, piece_in, (((1,), (1,)), ((), ())), preferred_element_type=jnp.float32
        )
        acts = gelu_tanh(pre).astype(jnp.bfloat16)
        grad_act = lax.dot_general(
            grads_in, piece_out, (((1,), (1,)), ((), ())), preferred_element_type=jnp.float32
        )
        dpre = (grad_act * gelu_slope(pre)).astype(jnp.bfloat16)
        part = jnp.dot(dpre, piece_in, preferred_element_type=jnp.float32)
        slot_sum = part if slot_sum is None else slot_sum + part
        term_in = lax.dot_general(
            dpre, rows_in, (((0,), (0,)), ((), ())), preferred_element_type=jnp.float32
        )
        term_out = lax.dot_general(
            acts, grads_in, (((0,), (0,)), ((), ())), preferred_element_type=jnp.float32
        )
        terms.append((term_in, term_out))
    returned = lax.all_to_all(
        slot_sum.astype(jnp.bfloat16).reshape(experts, capacity, model_width),
        "expert",
        split_axis=0,
        concat_axis=0,
        tiled=True,
    )
    token_grads = lax.dot_general(
        route_mat,
        returned.reshape(slot_rows, model_width),
        (((0,), (0,)), ((), ())),
        preferred_element_type=jnp.float32,
    )
    d_tokens = token_grads.astype(jnp.bfloat16)
    grid_shape = (nx, ny, half, model_width)
    sums_in, sums_out = [], []
    for h in range(2):
        term_in = terms[h][0].astype(jnp.bfloat16).reshape(grid_shape)
        term_out = terms[h][1].astype(jnp.bfloat16).reshape(grid_shape)
        sums_in.append(grid_reduce(term_in, ny, nx, *STREAMS[h])[0])
        total, tied = grid_reduce(term_out, ny, nx, *STREAMS[2 + h], companion=d_tokens if h else None)
        sums_out.append(total)
        if h:
            d_tokens = tied
    grad_in = jnp.concatenate(sums_in, axis=0)[None]
    grad_out = jnp.concatenate(sums_out, axis=0)[None]
    return (d_tokens, grad_in, grad_out)


def solution(mesh):
    in_specs = (
        P(("dp", "expert"), None),
        P(("dp", "expert"), None),
        P(("dp", "expert"), None),
        P(("dp", "expert"), None),
        P("expert", "dp", None),
        P("expert", "dp", None),
    )
    out_specs = (P(("dp", "expert"), None), P("expert", "dp", None), P("expert", "dp", None))
    return jax.shard_map(shards, mesh=mesh, in_specs=in_specs, out_specs=out_specs, check_vma=False)
```

```python
import jax
import jax.numpy as jnp
from jax import lax
from jax.sharding import PartitionSpec as P

tanh_coef = 0.7978845608028654
cubic_coef = 0.044715


def gelu_tanh(value):
    inner = tanh_coef * (value + cubic_coef * value * value * value)
    return 0.5 * value * (1.0 + jnp.tanh(inner))


def gelu_slope(value):
    inner = tanh_coef * (value + cubic_coef * value * value * value)
    slope_t = jnp.tanh(inner)
    return 0.5 * (1.0 + slope_t) + 0.5 * value * (1.0 - slope_t * slope_t) * tanh_coef * (
        1.0 + 3.0 * cubic_coef * value * value
    )


def dispatch_tables(route_blk, gate_blk, experts, capacity):
    tok_rows = route_blk.shape[0]
    flat = route_blk.reshape(-1)
    onehot = (flat[:, None] == jnp.arange(experts, dtype=jnp.int32)[None, :]).astype(jnp.int32)
    before = jnp.cumsum(onehot, axis=0) - onehot
    position = jnp.sum(before * onehot, axis=1)
    slots = (flat * capacity + position).reshape(tok_rows, -1)
    slot_ids = jnp.arange(experts * capacity, dtype=jnp.int32)
    placed = slot_ids[:, None, None] == slots[None, :, :]
    route_mat = jnp.sum(placed.astype(jnp.int32), axis=2).astype(jnp.bfloat16)
    gate_slot = jnp.sum(jnp.where(placed, gate_blk[None, :, :], jnp.float32(0.0)), axis=(1, 2))
    return (route_mat, gate_slot)


def grid_perm(ny, nx, dim, sign):
    pairs = []
    for d in range(ny * nx):
        cy, cx = divmod(d, nx)
        if dim == "x":
            pairs.append((d, cy * nx + (cx + sign) % nx))
        else:
            pairs.append((d, ((cy + sign) % ny) * nx + cx))
    return pairs


def ring_gather(piece, n, perm, sign):
    got = [None] * n
    got[0] = piece
    cur = piece
    for s in range(n - 1):
        cur = lax.ppermute(cur, "dp", perm)
        got[(sign * (s + 1)) % n] = cur
    return jnp.stack(got)


def grid_gather(piece, ny, nx, first, second):
    sizes = {"x": nx, "y": ny}
    g1 = ring_gather(piece, sizes[first[0]], grid_perm(ny, nx, *first), first[1])
    g2 = ring_gather(g1, sizes[second[0]], grid_perm(ny, nx, *second), second[1])
    if first[0] == "x":
        g2 = jnp.swapaxes(g2, 0, 1)
    return g2


def ring_reduce(blocks, n, perm, sign):
    acc = blocks[sign % n]
    for s in range(n - 1):
        recv = lax.ppermute(acc.astype(jnp.bfloat16), "dp", perm)
        acc = recv.astype(jnp.float32) + blocks[(sign * (s + 2)) % n].astype(jnp.float32)
    return acc


def grid_reduce(term, ny, nx, first, second):
    sizes = {"x": nx, "y": ny}
    n1, n2 = sizes[first[0]], sizes[second[0]]
    if first[0] == "x":
        blocks = [term[k] for k in range(n1)]
    else:
        blocks = [term[:, k] for k in range(n1)]
    part = ring_reduce(blocks, n1, grid_perm(ny, nx, *first), first[1])
    return ring_reduce([part[k] for k in range(n2)], n2, grid_perm(ny, nx, *second), second[1])


STREAMS = ((("x", 1), ("y", 1)), (("x", -1), ("y", -1)), (("y", 1), ("x", 1)), (("y", -1), ("x", -1)))


def shards(tokens, cotangent, routes, gates, w_in, w_out):
    experts = lax.axis_size("expert")
    tok_rows, model_width = tokens.shape
    top_count = routes.shape[1]
    capacity = 3 * tok_rows * top_count // experts
    shard_rows = w_in.shape[1]
    slot_rows = experts * capacity
    route_mat, gate_slot = dispatch_tables(routes, gates, experts, capacity)
    paired = jnp.dot(
        route_mat, jnp.concatenate([tokens, cotangent], axis=1), preferred_element_type=jnp.float32
    )
    scale = jnp.concatenate(
        [jnp.ones((slot_rows, model_width), jnp.float32), jnp.broadcast_to(gate_slot[:, None], (slot_rows, model_width))],
        axis=1,
    )
    both_sent = (paired * scale).astype(jnp.bfloat16).reshape(experts, capacity, 2 * model_width)
    both_recv = lax.all_to_all(both_sent, "expert", split_axis=0, concat_axis=0, tiled=True)
    rows_in = both_recv[:, :, :model_width].reshape(slot_rows, model_width)
    grads_in = both_recv[:, :, model_width:].reshape(slot_rows, model_width)
    n_dp = lax.axis_size("dp")
    nx = 4 if n_dp % 4 == 0 else 1
    ny = n_dp // nx
    half = shard_rows // 2
    halves = []
    for h in range(2):
        rows_h = slice(h * half, (h + 1) * half)
        in_h = grid_gather(w_in[0][rows_h], ny, nx, *STREAMS[h])
        out_h = grid_gather(w_out[0][rows_h], ny, nx, *STREAMS[2 + h])
        halves.append((in_h.reshape(-1, model_width), out_h.reshape(-1, model_width)))
    slot_sum = None
    terms = []
    for piece_in, piece_out in halves:
        pre = lax.dot_general(
            rows_in, piece_in, (((1,), (1,)), ((), ())), preferred_element_type=jnp.float32
        )
        acts = gelu_tanh(pre).astype(jnp.bfloat16)
        grad_act = lax.dot_general(
            grads_in, piece_out, (((1,), (1,)), ((), ())), preferred_element_type=jnp.float32
        )
        dpre = (grad_act * gelu_slope(pre)).astype(jnp.bfloat16)
        part = jnp.dot(dpre, piece_in, preferred_element_type=jnp.float32)
        slot_sum = part if slot_sum is None else slot_sum + part
        term_in = lax.dot_general(
            dpre, rows_in, (((0,), (0,)), ((), ())), preferred_element_type=jnp.float32
        )
        term_out = lax.dot_general(
            acts, grads_in, (((0,), (0,)), ((), ())), preferred_element_type=jnp.float32
        )
        terms.append((term_in, term_out))
    returned = lax.all_to_all(
        slot_sum.astype(jnp.bfloat16).reshape(experts, capacity, model_width),
        "expert",
        split_axis=0,
        concat_axis=0,
        tiled=True,
    )
    token_grads = lax.dot_general(
        route_mat,
        returned.reshape(slot_rows, model_width),
        (((0,), (0,)), ((), ())),
        preferred_element_type=jnp.float32,
    )
    d_tokens = token_grads.astype(jnp.bfloat16)
    grid_shape = (nx, ny, half, model_width)
    sums_in, sums_out = [], []
    for h in range(2):
        term_in = terms[h][0].astype(jnp.bfloat16).reshape(grid_shape)
        term_out = terms[h][1].astype(jnp.bfloat16).reshape(grid_shape)
        sums_in.append(grid_reduce(term_in, ny, nx, *STREAMS[h]))
        sums_out.append(grid_reduce(term_out, ny, nx, *STREAMS[2 + h]))
    grad_in = jnp.concatenate(sums_in, axis=0)[None]
    grad_out = jnp.concatenate(sums_out, axis=0)[None]
    return (d_tokens, grad_in, grad_out)


def solution(mesh):
    in_specs = (
        P(("dp", "expert"), None),
        P(("dp", "expert"), None),
        P(("dp", "expert"), None),
        P(("dp", "expert"), None),
        P("expert", "dp", None),
        P("expert", "dp", None),
    )
    out_specs = (P(("dp", "expert"), None), P("expert", "dp", None), P("expert", "dp", None))
    return jax.shard_map(shards, mesh=mesh, in_specs=in_specs, out_specs=out_specs, check_vma=False)
```
